32 devices in a mesh: gx: 4 (over x, core), gy: 8 (over z, y).
Axes of the slice: x: 2, y: 2, z: 4, core: 2. Of those that a mesh axis runs over, the one named last changes fastest.
Arguments:
- c_upper: bfloat16 [4, 8, 96, 96], P('gx', 'gy'), may hold values from -60 to 60
- edge_upper: bfloat16 [4, 8, 96, 1536], P('gx', 'gy'), may hold values from -60 to 60
- edge_left: bfloat16 [4, 8, 96, 1536], P('gx', 'gy'), may hold values from -60 to 60
- c_lower: bfloat16 [4, 8, 96, 96], P('gx', 'gy'), may hold values from -60 to 60
- edge_lower: bfloat16 [4, 8, 96, 1536], P('gx', 'gy'), may hold values from -60 to 60
- site_ket: bfloat16 [4, 8, 2, 256], P('gx', 'gy'), may hold values from -6 to 6
- time_gate: float32 [2, 2], replicated, may hold values from -3 to 3
- quench_sites: int32 [4], replicated, may hold values from 0 to 31
Outputs:
- new_c_upper: bfloat16 [4, 8, 96, 96], P('gx', 'gy')
- new_edge_left: bfloat16 [4, 8, 96, 1536], P('gx', 'gy')
- new_c_lower: bfloat16 [4, 8, 96, 96], P('gx', 'gy')
The draws below stay inside these ranges and needn't reach their ends.
All inputs are finite; a program needn't handle non-finite values.
Results may differ from the reference program's by a relative error of at most 0.03.
Values may be sent and summed in bfloat16 or wider, within the bound.
No kernel may reach another device: no remote copies, remote signals or barrier semaphores. Data moves between devices by JAX's collectives and lax.ppermute only.
A program may use at most 64 MiB of HBM per device.

```python
import math
import jax
import jax.numpy as jnp
from jax import lax

CHI = 96
BOND = 4
PHYS = 2
NS_ITERS = 6
STEPS = 2
QUENCH = 4
B = 16
NCOL = 4
NROW = 8


def scaled_entries(key, rows, cols):
    base_key, row_key, col_key = jax.random.split(key, 3)
    shape = (NCOL, NROW, rows, cols)
    base = jnp.clip(jax.random.normal(base_key, shape, jnp.float32), -6.0, 6.0)
    top = math.log(10.0)
    row_scale = jnp.exp(jax.random.uniform(row_key, (NCOL, NROW, rows, 1), jnp.float32, 0.0, top))
    col_scale = jnp.exp(jax.random.uniform(col_key, (NCOL, NROW, 1, cols), jnp.float32, 0.0, top))
    return (base * row_scale * col_scale * 0.1).astype(jnp.bfloat16)


def draw_c_upper(key, part):
    return scaled_entries(jax.random.fold_in(key, 11), CHI, CHI)


def draw_edge_upper(key, part):
    return scaled_entries(jax.random.fold_in(key, 12), CHI, B * CHI)


def draw_edge_left(key, part):
    return scaled_entries(jax.random.fold_in(key, 13), CHI, B * CHI)


def draw_c_lower(key, part):
    return scaled_entries(jax.random.fold_in(key, 14), CHI, CHI)


def draw_edge_lower(key, part):
    return scaled_entries(jax.random.fold_in(key, 15), CHI, B * CHI)


def place_ends(result, rng, low, high):
    place = [jax.random.randint(jax.random.fold_in(rng, axis), (), 0, length) for axis, length in enumerate(result.shape)]
    widest = result.shape.index(max(result.shape))
    neighbour = place[:widest] + [(place[widest] + 1) % result.shape[widest]] + place[widest + 1:]
    return result.at[tuple(place)].set(low).at[tuple(neighbour)].set(high)


def shard_levels(stream_key, extent, pieces, smallest, high):
    def one(axis_at, parts):
        draws = jax.random.uniform(jax.random.fold_in(jax.random.fold_in(stream_key, 6), axis_at), (parts,), jnp.float32, smallest / len(pieces), high / len(pieces))
        return jnp.repeat(jnp.exp(draws), extent[axis_at] // parts).reshape((-1,) + (1,) * (len(extent) - axis_at - 1))

    gain = one(*pieces[0])
    for cut in pieces[1:]:
        gain = gain * one(*cut)
    return gain


def normal_values(rng, shape, deviation, bound, pieces=(), kind=jnp.bfloat16):
    factor_of = shard_levels(rng, shape, pieces, -0.22, 0.18) if pieces else 1.0
    entries = jax.random.normal(rng, shape, jnp.float32) * deviation * factor_of
    return jnp.minimum(jnp.maximum(entries, -bound), bound).astype(kind)


def setup_inputs(seed: int = 0) -> dict:
    keys = jax.random.split(jax.random.key(seed), 9)
    return {
        "c_upper": draw_c_upper(jax.random.fold_in(keys[8], 71), 0),
        "edge_upper": draw_edge_upper(jax.random.fold_in(keys[8], 71), 0),
        "edge_left": draw_edge_left(jax.random.fold_in(keys[8], 71), 0),
        "c_lower": draw_c_lower(jax.random.fold_in(keys[8], 71), 0),
        "edge_lower": draw_edge_lower(jax.random.fold_in(keys[8], 71), 0),
        "site_ket": normal_values(keys[5], (NCOL, NROW, PHYS, BOND * BOND * BOND * BOND), 1.0, 6.0, ((0, 4), (1, 8))),
        "time_gate": normal_values(keys[6], (PHYS, PHYS), 1.0, 3.0, (), jnp.float32),
        "quench_sites": place_ends(jax.random.randint(keys[7], (QUENCH,), 0, NCOL * NROW), jax.random.fold_in(keys[7], 1), 0, (NCOL * NROW) - 1).astype(jnp.int32),
    }


def polar_factor(matrix):
    scale = jnp.sqrt(jnp.sum(matrix * matrix) + 1e-06)
    iterate = matrix / scale
    for sweep in range(NS_ITERS):
        gram = jnp.dot(iterate.T, iterate, precision=lax.Precision.HIGHEST)
        iterate = 1.5 * iterate - 0.5 * jnp.dot(iterate, gram, precision=lax.Precision.HIGHEST)
    return iterate

def unit_scaled(tensor):
    return tensor / jnp.sqrt(jnp.mean(tensor * tensor) + 1e-06)

def absorb_column(columns):
    corner_in, west_in, lower_in, north_edge, south_edge, ket_col, bra_col = columns
    upper = jnp.einsum('yab,ybc->yac', corner_in.astype(jnp.float32), north_edge.astype(jnp.float32)).reshape(NROW, CHI * B, CHI)
    lower = jnp.einsum('yab,ybc->yac', lower_in.astype(jnp.float32), south_edge.astype(jnp.float32)).reshape(NROW, CHI * B, CHI)
    proj_below = jax.vmap(polar_factor)(lower + jnp.roll(upper, -1, axis=0))
    proj_above = jnp.roll(proj_below, 1, axis=0)
    corner_up = jnp.einsum('yri,yrc->yic', proj_above, upper, precision=lax.Precision.HIGHEST)
    corner_low = jnp.einsum('yri,yrc->yic', proj_below, lower, precision=lax.Precision.HIGHEST)
    corner_up = jax.vmap(unit_scaled)(corner_up).astype(jnp.bfloat16)
    corner_low = jax.vmap(unit_scaled)(corner_low).astype(jnp.bfloat16)
    low_half = proj_below.astype(jnp.bfloat16).astype(jnp.float32).reshape(NROW, CHI, B, CHI)
    up_half = proj_above.astype(jnp.bfloat16).astype(jnp.float32).reshape(NROW, CHI, BOND, BOND, CHI)
    west = west_in.astype(jnp.float32).reshape(NROW, CHI, B, CHI)
    first = jnp.einsum('yulw,ywdj->yuldj', west, low_half).astype(jnp.bfloat16)
    first = first.reshape(NROW, CHI, BOND, BOND, BOND, BOND, CHI)
    second = jnp.einsum('yuaebfj,ysagcb->yuefjsgc', first.astype(jnp.float32), ket_col.astype(jnp.float32)).astype(jnp.bfloat16)
    third = jnp.einsum('yuefjsgc,ysehkf->yughckj', second.astype(jnp.float32), bra_col.astype(jnp.float32)).astype(jnp.bfloat16)
    edge_new = jnp.einsum('yughi,yughckj->yickj', up_half, third.astype(jnp.float32)).reshape(NROW, CHI, B * CHI)
    edge_new = jax.vmap(unit_scaled)(edge_new).astype(jnp.bfloat16)
    return (corner_up, edge_new, corner_low)

def reference(c_upper, edge_upper, edge_left, c_lower, edge_lower, site_ket, time_gate, quench_sites):
    ket_wide = site_ket.astype(jnp.float32).reshape(NCOL, NROW, PHYS, BOND, BOND, BOND, BOND)
    gram = jnp.dot(time_gate.T, time_gate, precision=lax.Precision.HIGHEST)
    gated = jnp.einsum('st,xytabcd->xysabcd', gram, ket_wide, precision=lax.Precision.HIGHEST)
    flat_index = (jnp.arange(NCOL, dtype=jnp.int32)[:, None] * NROW + jnp.arange(NROW, dtype=jnp.int32)[None, :]).astype(jnp.int32)
    hit_any = jnp.any(flat_index[:, :, None] == quench_sites.astype(jnp.int32)[None, None, :], axis=-1)
    chosen = hit_any[:, :, None, None, None, None, None]
    bra = jnp.where(chosen, gated, ket_wide).astype(jnp.bfloat16)
    ket_sites = site_ket.reshape(NCOL, NROW, PHYS, BOND, BOND, BOND, BOND)
    corner_up, west_edge, corner_low = (c_upper, edge_left, c_lower)
    for step in range(STEPS):
        fresh = lax.map(absorb_column, (corner_up, west_edge, corner_low, edge_upper, edge_lower, ket_sites, bra))
        corner_up = jnp.roll(fresh[0], 1, axis=0)
        west_edge = jnp.roll(fresh[1], 1, axis=0)
        corner_low = jnp.roll(fresh[2], 1, axis=0)
    return (corner_up, west_edge, corner_low)
```

```python
import math

import jax
import jax.numpy as jnp
from jax import lax
from jax.experimental import pallas as pl
from jax.experimental.pallas import tpu as pltpu
from jax.sharding import PartitionSpec as P

NS_ITERS = 6
STEPS = 2
LANES = 128


def passed_along(shard, axis, by):
    peers = lax.axis_size(axis)
    return lax.ppermute(shard, axis, [(i, (i + by) % peers) for i in range(peers)])


def polar_factor(matrix):
    scale = jnp.sqrt(jnp.sum(matrix * matrix) + 1e-06)
    iterate = matrix / scale
    for sweep in range(NS_ITERS):
        gram = jnp.dot(iterate.T, iterate, precision=lax.Precision.HIGHEST)
        iterate = 1.5 * iterate - 0.5 * jnp.dot(iterate, gram, precision=lax.Precision.HIGHEST)
    return iterate


def unit_scaled(tensor):
    return tensor / jnp.sqrt(jnp.mean(tensor * tensor) + 1e-06)


def edge_kernel(wd_ref, pm_ref, t_ref, qt_ref, o_ref, f_ref, g_ref):
    n = qt_ref.shape[0]
    dd = o_ref.shape[0]
    ub = 8

    def first_body(b, carry):
        rows = wd_ref[pl.ds(pl.multiple_of(b * ub * dd, ub * dd), ub * dd), :]
        for d in range(dd):
            part = jnp.dot(rows, pm_ref[:, d * LANES:(d + 1) * LANES], preferred_element_type=jnp.float32)
            f_ref[pl.ds(pl.multiple_of(b * ub, ub), ub), d] = part.astype(jnp.bfloat16).reshape(ub, dd, LANES)
        return carry

    lax.fori_loop(0, n // ub, first_body, 0)
    t = t_ref[...]

    def mid_body(h, carry):
        x = jnp.concatenate([f_ref[h * 2 + k].reshape(dd * dd, LANES) for k in range(2)], axis=1)
        g = jnp.dot(t, x, preferred_element_type=jnp.float32).astype(jnp.bfloat16)
        for k in range(2):
            at = pl.multiple_of((h * 2 + k) * dd, dd)
            for r in range(dd):
                g_ref[pl.ds(at, dd), r * LANES:(r + 1) * LANES] = g[r * dd:(r + 1) * dd, k * LANES:(k + 1) * LANES]
        return carry

    lax.fori_loop(0, n // 2, mid_body, 0)
    qt = qt_ref[...]
    for r in range(dd):
        o_ref[r] = jnp.dot(qt, g_ref[:, r * LANES:(r + 1) * LANES], preferred_element_type=jnp.float32)


def edge_contract(west, low_half, up_half, site):
    n = west.shape[0]
    dd = west.shape[1] // n
    wd = west.reshape(n * dd, n)
    pm = jnp.pad(low_half.reshape(n, dd, n), ((0, 0), (0, 0), (0, LANES - n))).reshape(n, dd * LANES)
    qt = up_half.T
    vmem = pltpu.MemorySpace.VMEM if hasattr(pltpu, "MemorySpace") else pltpu.VMEM
    out = pl.pallas_call(
        edge_kernel,
        out_shape=jax.ShapeDtypeStruct((dd, n, LANES), jnp.float32),
        scratch_shapes=[
            pltpu.VMEM((n, dd, dd, LANES), jnp.bfloat16),
            pltpu.VMEM((n * dd, dd * LANES), jnp.bfloat16),
        ],
        compiler_params=pltpu.CompilerParams(vmem_limit_bytes=48 * 1024 * 1024),
    )(wd, pm, site, qt)
    return jnp.transpose(out[:, :, :n], (1, 0, 2)).reshape(n, dd * n)


def per_device(
    c_upper, edge_upper, edge_left, c_lower, edge_lower, site_ket, time_gate, quench_sites
):
    env_width = c_upper.shape[-1]
    double_bond = edge_upper.shape[-1] // env_width
    bond_dim = math.isqrt(double_bond)
    phys_dim = site_ket.shape[2]
    ket_sites = site_ket[0, 0].reshape(phys_dim, bond_dim, bond_dim, bond_dim, bond_dim)
    gram = jnp.dot(time_gate.T, time_gate, precision=lax.Precision.HIGHEST)
    gated = jnp.einsum(
        "st,tabcd->sabcd", gram, ket_sites.astype(jnp.float32), precision=lax.Precision.HIGHEST
    )
    own_index = lax.axis_index("gx") * lax.axis_size("gy") + lax.axis_index("gy")
    chosen = jnp.any(quench_sites == own_index)
    bra = jnp.where(chosen, gated, ket_sites.astype(jnp.float32)).astype(jnp.bfloat16)
    site = jnp.einsum(
        "sagcb,sehkf->ckghbfae", ket_sites.astype(jnp.float32), bra.astype(jnp.float32),
        precision=lax.Precision.HIGHEST,
    ).reshape(double_bond * double_bond, double_bond * double_bond).astype(jnp.bfloat16)
    north_edge = edge_upper[0, 0]
    south_edge = edge_lower[0, 0]
    corner_up = c_upper[0, 0]
    west_edge = edge_left[0, 0]
    corner_low = c_lower[0, 0]
    for step in range(STEPS):
        upper = jnp.dot(corner_up, north_edge, preferred_element_type=jnp.float32).reshape(
            env_width * double_bond, env_width
        )
        lower = jnp.dot(corner_low, south_edge, preferred_element_type=jnp.float32).reshape(
            env_width * double_bond, env_width
        )
        from_below = passed_along(upper.astype(jnp.bfloat16), "gy", -1).astype(upper.dtype)
        proj_below = polar_factor(lower + from_below)
        proj_above = passed_along(proj_below.astype(jnp.bfloat16), "gy", 1).astype(proj_below.dtype)
        edge_new = edge_contract(
            west_edge, proj_below.astype(jnp.bfloat16), proj_above.astype(jnp.bfloat16), site
        )
        edge_new = unit_scaled(edge_new).astype(jnp.bfloat16)
        new_up = jnp.dot(proj_above.T, upper, precision=lax.Precision.HIGHEST)
        new_low = jnp.dot(proj_below.T, lower, precision=lax.Precision.HIGHEST)
        new_up = unit_scaled(new_up).astype(jnp.bfloat16)
        new_low = unit_scaled(new_low).astype(jnp.bfloat16)
        corner_up, west_edge, corner_low = passed_along((new_up, edge_new, new_low), "gx", 1)
    return (corner_up[None, None], west_edge[None, None], corner_low[None, None])


def solution(mesh):
    return jax.shard_map(
        per_device,
        mesh=mesh,
        in_specs=(
            P("gx", "gy", None, None),
            P("gx", "gy", None, None),
            P("gx", "gy", None, None),
            P("gx", "gy", None, None),
            P("gx", "gy", None, None),
            P("gx", "gy", None, None),
            P(),
            P(),
        ),
        out_specs=(P("gx", "gy", None, None), P("gx", "gy", None, None), P("gx", "gy", None, None)),
        check_vma=False,
    )
```

```python
import math

import jax
import jax.numpy as jnp
from jax import lax
from jax.experimental import pallas as pl
from jax.experimental.pallas import tpu as pltpu
from jax.sharding import PartitionSpec as P

NS_ITERS = 6
STEPS = 2
LANES = 128


def passed_along(shard, axis, by):
    peers = lax.axis_size(axis)
    return lax.ppermute(shard, axis, [(i, (i + by) % peers) for i in range(peers)])


def polar_factor(matrix):
    scale = jnp.sqrt(jnp.sum(matrix * matrix) + 1e-06)
    iterate = matrix / scale
    for sweep in range(NS_ITERS):
        gram = jnp.dot(iterate.T, iterate, precision=lax.Precision.HIGHEST)
        iterate = 1.5 * iterate - 0.5 * jnp.dot(iterate, gram, precision=lax.Precision.HIGHEST)
    return iterate


def unit_scaled(tensor):
    return tensor / jnp.sqrt(jnp.mean(tensor * tensor) + 1e-06)


def edge_kernel(wd_ref, pm_ref, t_ref, qt_ref, o_ref, f_ref, g_ref):
    n = qt_ref.shape[0]
    dd = o_ref.shape[0]

    wd = wd_ref[...]
    for d in range(dd):
        part = jnp.dot(wd, pm_ref[:, d * LANES:(d + 1) * LANES], preferred_element_type=jnp.float32)
        f_ref[:, d] = part.astype(jnp.bfloat16).reshape(n, dd, LANES)
    t = t_ref[...]

    def mid_body(h, carry):
        x = jnp.concatenate([f_ref[h * 2 + k].reshape(dd * dd, LANES) for k in range(2)], axis=1)
        g = jnp.dot(t, x, preferred_element_type=jnp.float32).astype(jnp.bfloat16)
        for k in range(2):
            at = pl.multiple_of((h * 2 + k) * dd, dd)
            for r in range(dd):
                g_ref[pl.ds(at, dd), r * LANES:(r + 1) * LANES] = g[r * dd:(r + 1) * dd, k * LANES:(k + 1) * LANES]
        return carry

    lax.fori_loop(0, n // 2, mid_body, 0)
    qt = qt_ref[...]
    for r in range(dd):
        o_ref[r] = jnp.dot(qt, g_ref[:, r * LANES:(r + 1) * LANES], preferred_element_type=jnp.float32)


def edge_contract(west, low_half, up_half, site):
    n = west.shape[0]
    dd = west.shape[1] // n
    wd = west.reshape(n * dd, n)
    pm = jnp.pad(low_half.reshape(n, dd, n), ((0, 0), (0, 0), (0, LANES - n))).reshape(n, dd * LANES)
    qt = up_half.T
    vmem = pltpu.MemorySpace.VMEM if hasattr(pltpu, "MemorySpace") else pltpu.VMEM
    out = pl.pallas_call(
        edge_kernel,
        out_shape=jax.ShapeDtypeStruct((dd, n, LANES), jnp.float32),
        scratch_shapes=[
            pltpu.VMEM((n, dd, dd, LANES), jnp.bfloat16),
            pltpu.VMEM((n * dd, dd * LANES), jnp.bfloat16),
        ],
        compiler_params=pltpu.CompilerParams(vmem_limit_bytes=48 * 1024 * 1024),
    )(wd, pm, site, qt)
    return jnp.transpose(out[:, :, :n], (1, 0, 2)).reshape(n, dd * n)


def one_hot(rows, cols, row_key, col_key):
    r = lax.broadcasted_iota(jnp.int32, (rows, cols), 0)
    c = lax.broadcasted_iota(jnp.int32, (rows, cols), 1)
    return (row_key(r) == col_key(c)).astype(jnp.float32)


def double_layer(ket, bra):
    q = ket.shape[1]
    dd = q * q
    size = dd * dd
    ket_m = jnp.transpose(ket.astype(jnp.float32), (0, 3, 2, 4, 1)).reshape(ket.shape[0], dd, dd)
    bra_m = jnp.transpose(bra.astype(jnp.float32), (0, 3, 2, 4, 1)).reshape(bra.shape[0], dd, dd)
    k_row = one_hot(size, dd, lambda r: (r // (q * dd)) * q + (r // q) % q, lambda c: c)
    b_row = one_hot(size, dd, lambda r: ((r // dd) % q) * q + r % q, lambda c: c)
    k_col = one_hot(dd, size, lambda r: r, lambda c: (c // (q * dd)) * q + (c // q) % q)
    b_col = one_hot(dd, size, lambda r: r, lambda c: ((c // dd) % q) * q + c % q)
    hi = lax.Precision.HIGHEST
    ket_wide = jnp.einsum("ra,sab,bc->src", k_row, ket_m, k_col, precision=hi)
    bra_wide = jnp.einsum("ra,sab,bc->src", b_row, bra_m, b_col, precision=hi)
    return jnp.sum(ket_wide * bra_wide, axis=0).astype(jnp.bfloat16)


def per_device(
    c_upper, edge_upper, edge_left, c_lower, edge_lower, site_ket, time_gate, quench_sites
):
    env_width = c_upper.shape[-1]
    double_bond = edge_upper.shape[-1] // env_width
    bond_dim = math.isqrt(double_bond)
    phys_dim = site_ket.shape[2]
    ket_sites = site_ket[0, 0].reshape(phys_dim, bond_dim, bond_dim, bond_dim, bond_dim)
    gram = jnp.dot(time_gate.T, time_gate, precision=lax.Precision.HIGHEST)
    gated = jnp.einsum(
        "st,tabcd->sabcd", gram, ket_sites.astype(jnp.float32), precision=lax.Precision.HIGHEST
    )
    own_index = lax.axis_index("gx") * lax.axis_size("gy") + lax.axis_index("gy")
    chosen = jnp.any(quench_sites == own_index)
    bra = jnp.where(chosen, gated, ket_sites.astype(jnp.float32)).astype(jnp.bfloat16)
    site = double_layer(ket_sites, bra)
    north_edge = edge_upper[0, 0]
    south_edge = edge_lower[0, 0]
    corner_up = c_upper[0, 0]
    west_edge = edge_left[0, 0]
    corner_low = c_lower[0, 0]
    for step in range(STEPS):
        upper = jnp.dot(corner_up, north_edge, preferred_element_type=jnp.float32).reshape(
            env_width * double_bond, env_width
        )
        lower = jnp.dot(corner_low, south_edge, preferred_element_type=jnp.float32).reshape(
            env_width * double_bond, env_width
        )
        from_below = passed_along(upper.astype(jnp.bfloat16), "gy", -1).astype(upper.dtype)
        proj_below = polar_factor(lower + from_below)
        proj_above = passed_along(proj_below.astype(jnp.bfloat16), "gy", 1).astype(proj_below.dtype)
        edge_new = edge_contract(
            west_edge, proj_below.astype(jnp.bfloat16), proj_above.astype(jnp.bfloat16), site
        )
        edge_new = unit_scaled(edge_new).astype(jnp.bfloat16)
        new_up = jnp.dot(proj_above.T, upper, precision=lax.Precision.HIGHEST)
        new_low = jnp.dot(proj_below.T, lower, precision=lax.Precision.HIGHEST)
        new_up = unit_scaled(new_up).astype(jnp.bfloat16)
        new_low = unit_scaled(new_low).astype(jnp.bfloat16)
        corner_up, west_edge, corner_low = passed_along((new_up, edge_new, new_low), "gx", 1)
    return (corner_up[None, None], west_edge[None, None], corner_low[None, None])


def solution(mesh):
    return jax.shard_map(
        per_device,
        mesh=mesh,
        in_specs=(
            P("gx", "gy", None, None),
            P("gx", "gy", None, None),
            P("gx", "gy", None, None),
            P("gx", "gy", None, None),
            P("gx", "gy", None, None),
            P("gx", "gy", None, None),
            P(),
            P(),
        ),
        out_specs=(P("gx", "gy", None, None), P("gx", "gy", None, None), P("gx", "gy", None, None)),
        check_vma=False,
    )
```

```python
import math

import jax
import jax.numpy as jnp
from jax import lax
from jax.experimental import pallas as pl
from jax.experimental.pallas import tpu as pltpu
from jax.sharding import PartitionSpec as P

NS_ITERS = 6
STEPS = 2
LANES = 128


def passed_along(shard, axis, by):
    peers = lax.axis_size(axis)
    return lax.ppermute(shard, axis, [(i, (i + by) % peers) for i in range(peers)])


def polar_factor(matrices):
    scale = jnp.sqrt(jnp.sum(matrices * matrices, axis=(1, 2), keepdims=True) + 1e-06)
    iterate = matrices / scale
    hi = lax.Precision.HIGHEST
    for sweep in range(NS_ITERS):
        gram = jnp.einsum("bri,brj->bij", iterate, iterate, precision=hi)
        iterate = 1.5 * iterate - 0.5 * jnp.einsum("bri,bij->brj", iterate, gram, precision=hi)
    return iterate


def shifted(tree, dx, dy):
    nx = lax.axis_size("gx")
    ny = lax.axis_size("gy")
    pairs = []
    for x in range(nx):
        for y in range(ny):
            pairs.append((x * ny + y, ((x + dx) % nx) * ny + (y + dy) % ny))
    return lax.ppermute(tree, ("gx", "gy"), pairs)


def unit_scaled(tensor):
    return tensor / jnp.sqrt(jnp.mean(tensor * tensor) + 1e-06)


def edge_kernel(wd_ref, pm_ref, t_ref, qt_ref, o_ref, f_ref, g_ref):
    n = qt_ref.shape[0]
    dd = o_ref.shape[0]

    wd = wd_ref[...]
    for d in range(dd):
        part = jnp.dot(wd, pm_ref[:, d * LANES:(d + 1) * LANES], preferred_element_type=jnp.float32)
        f_ref[:, d] = part.astype(jnp.bfloat16).reshape(n, dd, LANES)
    t = t_ref[...]

    def mid_body(h, carry):
        x = jnp.concatenate([f_ref[h * 2 + k].reshape(dd * dd, LANES) for k in range(2)], axis=1)
        g = jnp.dot(t, x, preferred_element_type=jnp.float32).astype(jnp.bfloat16)
        for k in range(2):
            at = pl.multiple_of((h * 2 + k) * dd, dd)
            for r in range(dd):
                g_ref[pl.ds(at, dd), r * LANES:(r + 1) * LANES] = g[r * dd:(r + 1) * dd, k * LANES:(k + 1) * LANES]
        return carry

    lax.fori_loop(0, n // 2, mid_body, 0)
    qt = qt_ref[...]
    for r in range(dd):
        o_ref[r] = jnp.dot(qt, g_ref[:, r * LANES:(r + 1) * LANES], preferred_element_type=jnp.float32)


def edge_contract(west, low_half, up_half, site):
    n = west.shape[0]
    dd = west.shape[1] // n
    wd = west.reshape(n * dd, n)
    pm = jnp.pad(low_half.reshape(n, dd, n), ((0, 0), (0, 0), (0, LANES - n))).reshape(n, dd * LANES)
    qt = up_half.T
    vmem = pltpu.MemorySpace.VMEM if hasattr(pltpu, "MemorySpace") else pltpu.VMEM
    out = pl.pallas_call(
        edge_kernel,
        out_shape=jax.ShapeDtypeStruct((dd, n, LANES), jnp.float32),
        scratch_shapes=[
            pltpu.VMEM((n, dd, dd, LANES), jnp.bfloat16),
            pltpu.VMEM((n * dd, dd * LANES), jnp.bfloat16),
        ],
        compiler_params=pltpu.CompilerParams(vmem_limit_bytes=48 * 1024 * 1024),
    )(wd, pm, site, qt)
    return jnp.transpose(out[:, :, :n], (1, 0, 2)).reshape(n, dd * n)


def one_hot(rows, cols, row_key, col_key):
    r = lax.broadcasted_iota(jnp.int32, (rows, cols), 0)
    c = lax.broadcasted_iota(jnp.int32, (rows, cols), 1)
    return (row_key(r) == col_key(c)).astype(jnp.float32)


def double_layer(ket, bra):
    q = ket.shape[1]
    dd = q * q
    size = dd * dd
    ket_m = jnp.transpose(ket.astype(jnp.float32), (0, 3, 2, 4, 1)).reshape(ket.shape[0], dd, dd)
    bra_m = jnp.transpose(bra.astype(jnp.float32), (0, 3, 2, 4, 1)).reshape(bra.shape[0], dd, dd)
    k_row = one_hot(size, dd, lambda r: (r // (q * dd)) * q + (r // q) % q, lambda c: c)
    b_row = one_hot(size, dd, lambda r: ((r // dd) % q) * q + r % q, lambda c: c)
    k_col = one_hot(dd, size, lambda r: r, lambda c: (c // (q * dd)) * q + (c // q) % q)
    b_col = one_hot(dd, size, lambda r: r, lambda c: ((c // dd) % q) * q + c % q)
    hi = lax.Precision.HIGHEST
    ket_wide = jnp.einsum("ra,sab,bc->src", k_row, ket_m, k_col, precision=hi)
    bra_wide = jnp.einsum("ra,sab,bc->src", b_row, bra_m, b_col, precision=hi)
    return jnp.sum(ket_wide * bra_wide, axis=0).astype(jnp.bfloat16)


def per_device(
    c_upper, edge_upper, edge_left, c_lower, edge_lower, site_ket, time_gate, quench_sites
):
    env_width = c_upper.shape[-1]
    double_bond = edge_upper.shape[-1] // env_width
    bond_dim = math.isqrt(double_bond)
    phys_dim = site_ket.shape[2]
    ket_sites = site_ket[0, 0].reshape(phys_dim, bond_dim, bond_dim, bond_dim, bond_dim)
    gram = jnp.dot(time_gate.T, time_gate, precision=lax.Precision.HIGHEST)
    gated = jnp.einsum(
        "st,tabcd->sabcd", gram, ket_sites.astype(jnp.float32), precision=lax.Precision.HIGHEST
    )
    own_index = lax.axis_index("gx") * lax.axis_size("gy") + lax.axis_index("gy")
    chosen = jnp.any(quench_sites == own_index)
    bra = jnp.where(chosen, gated, ket_sites.astype(jnp.float32)).astype(jnp.bfloat16)
    site = double_layer(ket_sites, bra)
    north_edge = edge_upper[0, 0]
    south_edge = edge_lower[0, 0]
    corner_up = c_upper[0, 0]
    west_edge = edge_left[0, 0]
    corner_low = c_lower[0, 0]
    up_corner_nb, north_nb = shifted((corner_up, north_edge), 0, -1)
    low_corner_nb, south_nb = shifted((corner_low, south_edge), 0, 1)
    n = env_width
    for step in range(STEPS):
        def half(corner, edge):
            return jnp.dot(corner, edge, preferred_element_type=jnp.float32).reshape(n * double_bond, n)

        upper = half(corner_up, north_edge)
        lower = half(corner_low, south_edge)
        upper_nb = half(up_corner_nb, north_nb)
        lower_nb = half(low_corner_nb, south_nb)
        projs = polar_factor(jnp.stack([lower + upper_nb, lower_nb + upper]))
        proj_below = projs[0]
        proj_above = projs[1].astype(jnp.bfloat16).astype(jnp.float32)
        new_up = jnp.dot(proj_above.T, upper, precision=lax.Precision.HIGHEST)
        new_low = jnp.dot(proj_below.T, lower, precision=lax.Precision.HIGHEST)
        new_up = unit_scaled(new_up).astype(jnp.bfloat16)
        new_low = unit_scaled(new_low).astype(jnp.bfloat16)
        if step + 1 < STEPS:
            up_corner_nb = shifted(new_up, 1, -1)
            low_corner_nb = shifted(new_low, 1, 1)
        edge_new = edge_contract(
            west_edge, proj_below.astype(jnp.bfloat16), proj_above.astype(jnp.bfloat16), site
        )
        edge_new = unit_scaled(edge_new).astype(jnp.bfloat16)
        corner_up, west_edge, corner_low = shifted((new_up, edge_new, new_low), 1, 0)
    return (corner_up[None, None], west_edge[None, None], corner_low[None, None])


def solution(mesh):
    return jax.shard_map(
        per_device,
        mesh=mesh,
        in_specs=(
            P("gx", "gy", None, None),
            P("gx", "gy", None, None),
            P("gx", "gy", None, None),
            P("gx", "gy", None, None),
            P("gx", "gy", None, None),
            P("gx", "gy", None, None),
            P(),
            P(),
        ),
        out_specs=(P("gx", "gy", None, None), P("gx", "gy", None, None), P("gx", "gy", None, None)),
        check_vma=False,
    )
```

```python
import math

import jax
import jax.numpy as jnp
from jax import lax
from jax.experimental import pallas as pl
from jax.experimental.pallas import tpu as pltpu
from jax.sharding import PartitionSpec as P

NS_ITERS = 6
STEPS = 2
LANES = 128


def passed_along(shard, axis, by):
    peers = lax.axis_size(axis)
    return lax.ppermute(shard, axis, [(i, (i + by) % peers) for i in range(peers)])


def split_bf16(x):
    hi = x.astype(jnp.bfloat16)
    return hi, (x - hi.astype(jnp.float32)).astype(jnp.bfloat16)


def dot3(a, b, dims):
    ah, al = split_bf16(a)
    bh, bl = split_bf16(b)
    out = lambda p, q: lax.dot_general(p, q, (dims, ((), ())), preferred_element_type=jnp.float32)
    return out(ah, bh) + (out(ah, bl) + out(al, bh))


def polar_kernel(y_ref, o_ref):
    count = y_ref.shape[0]
    ys = []
    for b in range(count):
        y = y_ref[b]
        ys.append(y / jnp.sqrt(jnp.sum(y * y) + 1e-06))
    for sweep in range(NS_ITERS):
        grams = [dot3(y, y, ((1,), (1,))) for y in ys]
        ys = [1.5 * y - 0.5 * dot3(g, y, ((1,), (0,))) for g, y in zip(grams, ys)]
    for b in range(count):
        o_ref[b] = ys[b]


def polar_factor_t(stack):
    return pl.pallas_call(
        polar_kernel,
        out_shape=jax.ShapeDtypeStruct(stack.shape, jnp.float32),
        compiler_params=pltpu.CompilerParams(vmem_limit_bytes=32 * 1024 * 1024),
    )(stack)


def shifted(tree, dx, dy):
    nx = lax.axis_size("gx")
    ny = lax.axis_size("gy")
    pairs = []
    for x in range(nx):
        for y in range(ny):
            pairs.append((x * ny + y, ((x + dx) % nx) * ny + (y + dy) % ny))
    return lax.ppermute(tree, ("gx", "gy"), pairs)


def unit_scaled(tensor):
    return tensor / jnp.sqrt(jnp.mean(tensor * tensor) + 1e-06)


def edge_kernel(wd_ref, pm_ref, t_ref, qt_ref, o_ref, f_ref, g_ref):
    n = qt_ref.shape[0]
    dd = o_ref.shape[0]

    wd = wd_ref[...]
    for d in range(dd):
        part = jnp.dot(wd, pm_ref[:, d * LANES:(d + 1) * LANES], preferred_element_type=jnp.float32)
        f_ref[:, d] = part.astype(jnp.bfloat16).reshape(n, dd, LANES)
    t = t_ref[...]

    def mid_body(h, carry):
        x = jnp.concatenate([f_ref[h * 2 + k].reshape(dd * dd, LANES) for k in range(2)], axis=1)
        g = jnp.dot(t, x, preferred_element_type=jnp.float32).astype(jnp.bfloat16)
        for k in range(2):
            at = pl.multiple_of((h * 2 + k) * dd, dd)
            for r in range(dd):
                g_ref[pl.ds(at, dd), r * LANES:(r + 1) * LANES] = g[r * dd:(r + 1) * dd, k * LANES:(k + 1) * LANES]
        return carry

    lax.fori_loop(0, n // 2, mid_body, 0)
    qt = qt_ref[...]
    for r in range(dd):
        o_ref[r] = jnp.dot(qt, g_ref[:, r * LANES:(r + 1) * LANES], preferred_element_type=jnp.float32)


def edge_contract(west, low_t, up_t, site):
    n = west.shape[0]
    dd = west.shape[1] // n
    wd = west.reshape(n * dd, n)
    pm = jnp.transpose(low_t.reshape(n, n, dd), (1, 2, 0))
    pm = jnp.pad(pm, ((0, 0), (0, 0), (0, LANES - n))).reshape(n, dd * LANES)
    qt = up_t
    out = pl.pallas_call(
        edge_kernel,
        out_shape=jax.ShapeDtypeStruct((dd, n, LANES), jnp.float32),
        scratch_shapes=[
            pltpu.VMEM((n, dd, dd, LANES), jnp.bfloat16),
            pltpu.VMEM((n * dd, dd * LANES), jnp.bfloat16),
        ],
        compiler_params=pltpu.CompilerParams(vmem_limit_bytes=48 * 1024 * 1024),
    )(wd, pm, site, qt)
    return jnp.transpose(out[:, :, :n], (1, 0, 2)).reshape(n, dd * n)


def one_hot(rows, cols, row_key, col_key):
    r = lax.broadcasted_iota(jnp.int32, (rows, cols), 0)
    c = lax.broadcasted_iota(jnp.int32, (rows, cols), 1)
    return (row_key(r) == col_key(c)).astype(jnp.float32)


def double_layer(ket, bra):
    q = ket.shape[1]
    dd = q * q
    size = dd * dd
    ket_m = jnp.transpose(ket.astype(jnp.float32), (0, 3, 2, 4, 1)).reshape(ket.shape[0], dd, dd)
    bra_m = jnp.transpose(bra.astype(jnp.float32), (0, 3, 2, 4, 1)).reshape(bra.shape[0], dd, dd)
    k_row = one_hot(size, dd, lambda r: (r // (q * dd)) * q + (r // q) % q, lambda c: c)
    b_row = one_hot(size, dd, lambda r: ((r // dd) % q) * q + r % q, lambda c: c)
    k_col = one_hot(dd, size, lambda r: r, lambda c: (c // (q * dd)) * q + (c // q) % q)
    b_col = one_hot(dd, size, lambda r: r, lambda c: ((c // dd) % q) * q + c % q)
    hi = lax.Precision.HIGHEST
    ket_wide = jnp.einsum("ra,sab,bc->src", k_row, ket_m, k_col, precision=hi)
    bra_wide = jnp.einsum("ra,sab,bc->src", b_row, bra_m, b_col, precision=hi)
    return jnp.sum(ket_wide * bra_wide, axis=0).astype(jnp.bfloat16)


def per_device(
    c_upper, edge_upper, edge_left, c_lower, edge_lower, site_ket, time_gate, quench_sites
):
    env_width = c_upper.shape[-1]
    double_bond = edge_upper.shape[-1] // env_width
    bond_dim = math.isqrt(double_bond)
    phys_dim = site_ket.shape[2]
    ket_sites = site_ket[0, 0].reshape(phys_dim, bond_dim, bond_dim, bond_dim, bond_dim)
    gram = jnp.dot(time_gate.T, time_gate, precision=lax.Precision.HIGHEST)
    gated = jnp.einsum(
        "st,tabcd->sabcd", gram, ket_sites.astype(jnp.float32), precision=lax.Precision.HIGHEST
    )
    own_index = lax.axis_index("gx") * lax.axis_size("gy") + lax.axis_index("gy")
    chosen = jnp.any(quench_sites == own_index)
    bra = jnp.where(chosen, gated, ket_sites.astype(jnp.float32)).astype(jnp.bfloat16)
    site = double_layer(ket_sites, bra)
    north_edge = edge_upper[0, 0]
    south_edge = edge_lower[0, 0]
    corner_up = c_upper[0, 0]
    west_edge = edge_left[0, 0]
    corner_low = c_lower[0, 0]
    up_corner_nb, north_nb = shifted((corner_up, north_edge), 0, -1)
    low_corner_nb, south_nb = shifted((corner_low, south_edge), 0, 1)
    n = env_width
    for step in range(STEPS):
        def half(corner, edge):
            return jnp.dot(corner, edge, preferred_element_type=jnp.float32).reshape(n * double_bond, n)

        upper = half(corner_up, north_edge)
        lower = half(corner_low, south_edge)
        upper_nb = half(up_corner_nb, north_nb)
        lower_nb = half(low_corner_nb, south_nb)
        projs = polar_factor_t(jnp.swapaxes(jnp.stack([lower + upper_nb, lower_nb + upper]), 1, 2))
        below_t = projs[0]
        above_t = projs[1]
        new_up = jnp.dot(above_t, upper, precision=lax.Precision.HIGHEST)
        new_low = jnp.dot(below_t, lower, precision=lax.Precision.HIGHEST)
        new_up = unit_scaled(new_up).astype(jnp.bfloat16)
        new_low = unit_scaled(new_low).astype(jnp.bfloat16)
        if step + 1 < STEPS:
            up_corner_nb = shifted(new_up, 1, -1)
            low_corner_nb = shifted(new_low, 1, 1)
        edge_new = edge_contract(west_edge, below_t.astype(jnp.bfloat16), above_t.astype(jnp.bfloat16), site)
        edge_new = unit_scaled(edge_new).astype(jnp.bfloat16)
        corner_up, west_edge, corner_low = shifted((new_up, edge_new, new_low), 1, 0)
    return (corner_up[None, None], west_edge[None, None], corner_low[None, None])


def solution(mesh):
    return jax.shard_map(
        per_device,
        mesh=mesh,
        in_specs=(
            P("gx", "gy", None, None),
            P("gx", "gy", None, None),
            P("gx", "gy", None, None),
            P("gx", "gy", None, None),
            P("gx", "gy", None, None),
            P("gx", "gy", None, None),
            P(),
            P(),
        ),
        out_specs=(P("gx", "gy", None, None), P("gx", "gy", None, None), P("gx", "gy", None, None)),
        check_vma=False,
    )
```

```python
import math

import jax
import jax.numpy as jnp
from jax import lax
from jax.experimental import pallas as pl
from jax.experimental.pallas import tpu as pltpu
from jax.sharding import PartitionSpec as P

NS_ITERS = 6
STEPS = 2
LANES = 128


def passed_along(shard, axis, by):
    peers = lax.axis_size(axis)
    return lax.ppermute(shard, axis, [(i, (i + by) % peers) for i in range(peers)])


def split_bf16(x):
    hi = x.astype(jnp.bfloat16)
    return hi, (x - hi.astype(jnp.float32)).astype(jnp.bfloat16)


def dot3(a, b, dims):
    ah, al = split_bf16(a)
    bh, bl = split_bf16(b)
    out = lambda p, q: lax.dot_general(p, q, (dims, ((), ())), preferred_element_type=jnp.float32)
    return out(ah, bh) + (out(ah, bl) + out(al, bh))


def polar_kernel(y_ref, o_ref):
    count = y_ref.shape[0]
    ys = []
    for b in range(count):
        y = y_ref[b]
        ys.append(y / jnp.sqrt(jnp.sum(y * y) + 1e-06))
    for sweep in range(NS_ITERS):
        grams = [dot3(y, y, ((1,), (1,))) for y in ys]
        ys = [1.5 * y - 0.5 * dot3(g, y, ((1,), (0,))) for g, y in zip(grams, ys)]
    for b in range(count):
        o_ref[b] = ys[b]


def polar_factor_t(stack):
    return pl.pallas_call(
        polar_kernel,
        out_shape=jax.ShapeDtypeStruct(stack.shape, jnp.float32),
        compiler_params=pltpu.CompilerParams(vmem_limit_bytes=32 * 1024 * 1024),
    )(stack)


def shifted(tree, dx, dy):
    nx = lax.axis_size("gx")
    ny = lax.axis_size("gy")
    pairs = []
    for x in range(nx):
        for y in range(ny):
            pairs.append((x * ny + y, ((x + dx) % nx) * ny + (y + dy) % ny))
    return lax.ppermute(tree, ("gx", "gy"), pairs)


def unit_scaled(tensor):
    return tensor / jnp.sqrt(jnp.mean(tensor * tensor) + 1e-06)


def edge_kernel(wd_ref, pm_ref, t_ref, qt_ref, o_ref, f_ref, g_ref):
    n = qt_ref.shape[0]
    dd = o_ref.shape[0]
    group = 4
    wd = wd_ref[...]
    for d0 in range(0, dd, group):
        part = jnp.dot(wd, pm_ref[:, d0 * LANES:(d0 + group) * LANES], preferred_element_type=jnp.float32)
        part = part.astype(jnp.bfloat16)
        for k in range(group):
            f_ref[:, d0 + k] = part[:, k * LANES:(k + 1) * LANES].reshape(n, dd, LANES)
    t = t_ref[...]
    per = math.gcd(n, 24)

    def mid_body(h, carry):
        x = jnp.concatenate([f_ref[h * per + k].reshape(dd * dd, LANES) for k in range(per)], axis=1)
        g = jnp.dot(t, x, preferred_element_type=jnp.float32).astype(jnp.bfloat16)
        for k in range(per):
            at = pl.multiple_of((h * per + k) * dd, dd)
            for r in range(dd):
                g_ref[pl.ds(at, dd), r * LANES:(r + 1) * LANES] = g[r * dd:(r + 1) * dd, k * LANES:(k + 1) * LANES]
        return carry

    lax.fori_loop(0, n // per, mid_body, 0)
    qt = qt_ref[...]
    for r0 in range(0, dd, group):
        part = jnp.dot(qt, g_ref[:, r0 * LANES:(r0 + group) * LANES], preferred_element_type=jnp.float32)
        for k in range(group):
            o_ref[r0 + k] = part[:, k * LANES:(k + 1) * LANES]


def edge_contract(west, low_t, up_t, site):
    n = west.shape[0]
    dd = west.shape[1] // n
    wd = west.reshape(n * dd, n)
    pm = jnp.transpose(low_t.reshape(n, n, dd), (1, 2, 0))
    pm = jnp.pad(pm, ((0, 0), (0, 0), (0, LANES - n))).reshape(n, dd * LANES)
    qt = up_t
    out = pl.pallas_call(
        edge_kernel,
        out_shape=jax.ShapeDtypeStruct((dd, n, LANES), jnp.float32),
        scratch_shapes=[
            pltpu.VMEM((n, dd, dd, LANES), jnp.bfloat16),
            pltpu.VMEM((n * dd, dd * LANES), jnp.bfloat16),
        ],
        compiler_params=pltpu.CompilerParams(vmem_limit_bytes=48 * 1024 * 1024),
    )(wd, pm, site, qt)
    return jnp.transpose(out[:, :, :n], (1, 0, 2)).reshape(n, dd * n)


def one_hot(rows, cols, row_key, col_key):
    r = lax.broadcasted_iota(jnp.int32, (rows, cols), 0)
    c = lax.broadcasted_iota(jnp.int32, (rows, cols), 1)
    return (row_key(r) == col_key(c)).astype(jnp.float32)


def double_layer(ket, bra):
    q = ket.shape[1]
    dd = q * q
    size = dd * dd
    ket_m = jnp.transpose(ket.astype(jnp.float32), (0, 3, 2, 4, 1)).reshape(ket.shape[0], dd, dd)
    bra_m = jnp.transpose(bra.astype(jnp.float32), (0, 3, 2, 4, 1)).reshape(bra.shape[0], dd, dd)
    k_row = one_hot(size, dd, lambda r: (r // (q * dd)) * q + (r // q) % q, lambda c: c)
    b_row = one_hot(size, dd, lambda r: ((r // dd) % q) * q + r % q, lambda c: c)
    k_col = one_hot(dd, size, lambda r: r, lambda c: (c // (q * dd)) * q + (c // q) % q)
    b_col = one_hot(dd, size, lambda r: r, lambda c: ((c // dd) % q) * q + c % q)
    hi = lax.Precision.HIGHEST
    ket_wide = jnp.einsum("ra,sab,bc->src", k_row, ket_m, k_col, precision=hi)
    bra_wide = jnp.einsum("ra,sab,bc->src", b_row, bra_m, b_col, precision=hi)
    return jnp.sum(ket_wide * bra_wide, axis=0).astype(jnp.bfloat16)


def per_device(
    c_upper, edge_upper, edge_left, c_lower, edge_lower, site_ket, time_gate, quench_sites
):
    env_width = c_upper.shape[-1]
    double_bond = edge_upper.shape[-1] // env_width
    bond_dim = math.isqrt(double_bond)
    phys_dim = site_ket.shape[2]
    ket_sites = site_ket[0, 0].reshape(phys_dim, bond_dim, bond_dim, bond_dim, bond_dim)
    gram = jnp.dot(time_gate.T, time_gate, precision=lax.Precision.HIGHEST)
    gated = jnp.einsum(
        "st,tabcd->sabcd", gram, ket_sites.astype(jnp.float32), precision=lax.Precision.HIGHEST
    )
    own_index = lax.axis_index("gx") * lax.axis_size("gy") + lax.axis_index("gy")
    chosen = jnp.any(quench_sites == own_index)
    bra = jnp.where(chosen, gated, ket_sites.astype(jnp.float32)).astype(jnp.bfloat16)
    site = double_layer(ket_sites, bra)
    north_edge = edge_upper[0, 0]
    south_edge = edge_lower[0, 0]
    corner_up = c_upper[0, 0]
    west_edge = edge_left[0, 0]
    corner_low = c_lower[0, 0]
    up_corner_nb, north_nb = shifted((corner_up, north_edge), 0, -1)
    low_corner_nb, south_nb = shifted((corner_low, south_edge), 0, 1)
    n = env_width
    for step in range(STEPS):
        def half(corner, edge):
            return jnp.dot(corner, edge, preferred_element_type=jnp.float32).reshape(n * double_bond, n)

        upper = half(corner_up, north_edge)
        lower = half(corner_low, south_edge)
        upper_nb = half(up_corner_nb, north_nb)
        lower_nb = half(low_corner_nb, south_nb)
        projs = polar_factor_t(jnp.swapaxes(jnp.stack([lower + upper_nb, lower_nb + upper]), 1, 2))
        below_t = projs[0]
        above_t = projs[1]
        new_up = jnp.dot(above_t, upper, precision=lax.Precision.HIGHEST)
        new_low = jnp.dot(below_t, lower, precision=lax.Precision.HIGHEST)
        new_up = unit_scaled(new_up).astype(jnp.bfloat16)
        new_low = unit_scaled(new_low).astype(jnp.bfloat16)
        if step + 1 < STEPS:
            up_corner_nb = shifted(new_up, 1, -1)
            low_corner_nb = shifted(new_low, 1, 1)
        edge_new = edge_contract(west_edge, below_t.astype(jnp.bfloat16), above_t.astype(jnp.bfloat16), site)
        edge_new = unit_scaled(edge_new).astype(jnp.bfloat16)
        corner_up, west_edge, corner_low = shifted((new_up, edge_new, new_low), 1, 0)
    return (corner_up[None, None], west_edge[None, None], corner_low[None, None])


def solution(mesh):
    return jax.shard_map(
        per_device,
        mesh=mesh,
        in_specs=(
            P("gx", "gy", None, None),
            P("gx", "gy", None, None),
            P("gx", "gy", None, None),
            P("gx", "gy", None, None),
            P("gx", "gy", None, None),
            P("gx", "gy", None, None),
            P(),
            P(),
        ),
        out_specs=(P("gx", "gy", None, None), P("gx", "gy", None, None), P("gx", "gy", None, None)),
        check_vma=False,
    )
```

```python
import math

import jax
import jax.numpy as jnp
from jax import lax
from jax.experimental import pallas as pl
from jax.experimental.pallas import tpu as pltpu
from jax.sharding import PartitionSpec as P

NS_ITERS = 6
STEPS = 2
LANES = 128


def passed_along(shard, axis, by):
    peers = lax.axis_size(axis)
    return lax.ppermute(shard, axis, [(i, (i + by) % peers) for i in range(peers)])


def split_bf16(x):
    hi = x.astype(jnp.bfloat16)
    return hi, (x - hi.astype(jnp.float32)).astype(jnp.bfloat16)


def dot3(a, b, dims):
    ah, al = split_bf16(a)
    bh, bl = split_bf16(b)
    out = lambda p, q: lax.dot_general(p, q, (dims, ((), ())), preferred_element_type=jnp.float32)
    return out(ah, bh) + (out(ah, bl) + out(al, bh))


def polar_kernel(y_ref, h_ref, p_ref, c_ref):
    count = y_ref.shape[0]
    ys = []
    for b in range(count):
        y = y_ref[b]
        ys.append(y / jnp.sqrt(jnp.sum(y * y) + 1e-06))
    for sweep in range(NS_ITERS):
        grams = [dot3(y, y, ((1,), (1,))) for y in ys]
        ys = [1.5 * y - 0.5 * dot3(g, y, ((1,), (0,))) for g, y in zip(grams, ys)]
    for b in range(count):
        p_ref[b] = ys[b].astype(p_ref.dtype)
        corner = dot3(ys[b], h_ref[b], ((1,), (0,)))
        c_ref[b] = (corner / jnp.sqrt(jnp.mean(corner * corner) + 1e-06)).astype(c_ref.dtype)


def polar_factor_t(stack, halves):
    count, n, _ = stack.shape
    return pl.pallas_call(
        polar_kernel,
        out_shape=(
            jax.ShapeDtypeStruct(stack.shape, jnp.bfloat16),
            jax.ShapeDtypeStruct((count, n, n), jnp.bfloat16),
        ),
        compiler_params=pltpu.CompilerParams(vmem_limit_bytes=32 * 1024 * 1024),
    )(stack, halves)


def shifted(tree, dx, dy):
    nx = lax.axis_size("gx")
    ny = lax.axis_size("gy")
    pairs = []
    for x in range(nx):
        for y in range(ny):
            pairs.append((x * ny + y, ((x + dx) % nx) * ny + (y + dy) % ny))
    return lax.ppermute(tree, ("gx", "gy"), pairs)


def unit_scaled(tensor):
    return tensor / jnp.sqrt(jnp.mean(tensor * tensor) + 1e-06)


def edge_kernel(wd_ref, pm_ref, t_ref, qt_ref, o_ref, f_ref, g_ref):
    n = qt_ref.shape[0]
    dd = o_ref.shape[0]
    group = 4
    wd = wd_ref[...]
    for d0 in range(0, dd, group):
        part = jnp.dot(wd, pm_ref[:, d0 * LANES:(d0 + group) * LANES], preferred_element_type=jnp.float32)
        part = part.astype(jnp.bfloat16)
        for k in range(group):
            f_ref[:, d0 + k] = part[:, k * LANES:(k + 1) * LANES].reshape(n, dd, LANES)
    t = t_ref[...]
    per = math.gcd(n, 24)

    def mid_body(h, carry):
        x = jnp.concatenate([f_ref[h * per + k].reshape(dd * dd, LANES) for k in range(per)], axis=1)
        g = jnp.dot(t, x, preferred_element_type=jnp.float32).astype(jnp.bfloat16)
        for k in range(per):
            at = pl.multiple_of((h * per + k) * dd, dd)
            for r in range(dd):
                g_ref[pl.ds(at, dd), r * LANES:(r + 1) * LANES] = g[r * dd:(r + 1) * dd, k * LANES:(k + 1) * LANES]
        return carry

    lax.fori_loop(0, n // per, mid_body, 0)
    qt = qt_ref[...]
    for r0 in range(0, dd, group):
        part = jnp.dot(qt, g_ref[:, r0 * LANES:(r0 + group) * LANES], preferred_element_type=jnp.float32)
        for k in range(group):
            o_ref[r0 + k] = part[:, k * LANES:(k + 1) * LANES]


def edge_contract(west, low_t, up_t, site):
    n = west.shape[0]
    dd = west.shape[1] // n
    wd = west.reshape(n * dd, n)
    pm = jnp.transpose(low_t.reshape(n, n, dd), (1, 2, 0))
    pm = jnp.pad(pm, ((0, 0), (0, 0), (0, LANES - n))).reshape(n, dd * LANES)
    qt = up_t
    out = pl.pallas_call(
        edge_kernel,
        out_shape=jax.ShapeDtypeStruct((dd, n, LANES), jnp.float32),
        scratch_shapes=[
            pltpu.VMEM((n, dd, dd, LANES), jnp.bfloat16),
            pltpu.VMEM((n * dd, dd * LANES), jnp.bfloat16),
        ],
        compiler_params=pltpu.CompilerParams(vmem_limit_bytes=48 * 1024 * 1024),
    )(wd, pm, site, qt)
    return jnp.transpose(out[:, :, :n], (1, 0, 2)).reshape(n, dd * n)


def one_hot(rows, cols, row_key, col_key):
    r = lax.broadcasted_iota(jnp.int32, (rows, cols), 0)
    c = lax.broadcasted_iota(jnp.int32, (rows, cols), 1)
    return (row_key(r) == col_key(c)).astype(jnp.float32)


def double_layer(ket, bra):
    q = ket.shape[1]
    dd = q * q
    size = dd * dd
    ket_m = jnp.transpose(ket.astype(jnp.float32), (0, 3, 2, 4, 1)).reshape(ket.shape[0], dd, dd)
    bra_m = jnp.transpose(bra.astype(jnp.float32), (0, 3, 2, 4, 1)).reshape(bra.shape[0], dd, dd)
    k_row = one_hot(size, dd, lambda r: (r // (q * dd)) * q + (r // q) % q, lambda c: c)
    b_row = one_hot(size, dd, lambda r: ((r // dd) % q) * q + r % q, lambda c: c)
    k_col = one_hot(dd, size, lambda r: r, lambda c: (c // (q * dd)) * q + (c // q) % q)
    b_col = one_hot(dd, size, lambda r: r, lambda c: ((c // dd) % q) * q + c % q)
    hi = lax.Precision.HIGHEST
    ket_wide = jnp.einsum("ra,sab,bc->src", k_row, ket_m, k_col, precision=hi)
    bra_wide = jnp.einsum("ra,sab,bc->src", b_row, bra_m, b_col, precision=hi)
    return jnp.sum(ket_wide * bra_wide, axis=0).astype(jnp.bfloat16)


def per_device(
    c_upper, edge_upper, edge_left, c_lower, edge_lower, site_ket, time_gate, quench_sites
):
    env_width = c_upper.shape[-1]
    double_bond = edge_upper.shape[-1] // env_width
    bond_dim = math.isqrt(double_bond)
    phys_dim = site_ket.shape[2]
    ket_sites = site_ket[0, 0].reshape(phys_dim, bond_dim, bond_dim, bond_dim, bond_dim)
    gram = jnp.dot(time_gate.T, time_gate, precision=lax.Precision.HIGHEST)
    gated = jnp.einsum(
        "st,tabcd->sabcd", gram, ket_sites.astype(jnp.float32), precision=lax.Precision.HIGHEST
    )
    own_index = lax.axis_index("gx") * lax.axis_size("gy") + lax.axis_index("gy")
    chosen = jnp.any(quench_sites == own_index)
    bra = jnp.where(chosen, gated, ket_sites.astype(jnp.float32)).astype(jnp.bfloat16)
    site = double_layer(ket_sites, bra)
    north_edge = edge_upper[0, 0]
    south_edge = edge_lower[0, 0]
    corner_up = c_upper[0, 0]
    west_edge = edge_left[0, 0]
    corner_low = c_lower[0, 0]
    up_corner_nb, north_nb = shifted((corner_up, north_edge), 0, -1)
    low_corner_nb, south_nb = shifted((corner_low, south_edge), 0, 1)
    n = env_width
    for step in range(STEPS):
        def half(corner, edge):
            return jnp.dot(corner, edge, preferred_element_type=jnp.float32).reshape(n * double_bond, n)

        upper = half(corner_up, north_edge)
        lower = half(corner_low, south_edge)
        upper_nb = half(up_corner_nb, north_nb)
        lower_nb = half(low_corner_nb, south_nb)
        projs, corners = polar_factor_t(
            jnp.swapaxes(jnp.stack([lower + upper_nb, lower_nb + upper]), 1, 2), jnp.stack([lower, upper])
        )
        below_t = projs[0]
        above_t = projs[1]
        new_low = corners[0]
        new_up = corners[1]
        if step + 1 < STEPS:
            up_corner_nb = shifted(new_up, 1, -1)
            low_corner_nb = shifted(new_low, 1, 1)
        edge_new = edge_contract(west_edge, below_t, above_t, site)
        edge_new = unit_scaled(edge_new).astype(jnp.bfloat16)
        corner_up, west_edge, corner_low = shifted((new_up, edge_new, new_low), 1, 0)
    return (corner_up[None, None], west_edge[None, None], corner_low[None, None])


def solution(mesh):
    return jax.shard_map(
        per_device,
        mesh=mesh,
        in_specs=(
            P("gx", "gy", None, None),
            P("gx", "gy", None, None),
            P("gx", "gy", None, None),
            P("gx", "gy", None, None),
            P("gx", "gy", None, None),
            P("gx", "gy", None, None),
            P(),
            P(),
        ),
        out_specs=(P("gx", "gy", None, None), P("gx", "gy", None, None), P("gx", "gy", None, None)),
        check_vma=False,
    )
```

```python
import math

import jax
import jax.numpy as jnp
from jax import lax
from jax.experimental import pallas as pl
from jax.experimental.pallas import tpu as pltpu
from jax.sharding import PartitionSpec as P

NS_ITERS = 6
STEPS = 2
LANES = 128


def passed_along(shard, axis, by):
    peers = lax.axis_size(axis)
    return lax.ppermute(shard, axis, [(i, (i + by) % peers) for i in range(peers)])


def split_bf16(x):
    hi = x.astype(jnp.bfloat16)
    return hi, (x - hi.astype(jnp.float32)).astype(jnp.bfloat16)


def dot3(a, b, dims):
    ah, al = split_bf16(a)
    bh, bl = split_bf16(b)
    out = lambda p, q: lax.dot_general(p, q, (dims, ((), ())), preferred_element_type=jnp.float32)
    return out(ah, bh) + (out(ah, bl) + out(al, bh))


def polar_kernel(y_ref, o_ref):
    count = y_ref.shape[0]
    ys = []
    for b in range(count):
        y = y_ref[b]
        ys.append(y / jnp.sqrt(jnp.sum(y * y) + 1e-06))
    for sweep in range(NS_ITERS):
        grams = [dot3(y, y, ((1,), (1,))) for y in ys]
        ys = [1.5 * y - 0.5 * dot3(g, y, ((1,), (0,))) for g, y in zip(grams, ys)]
    for b in range(count):
        o_ref[b] = ys[b]


def polar_factor_t(stack):
    return pl.pallas_call(
        polar_kernel,
        out_shape=jax.ShapeDtypeStruct(stack.shape, jnp.float32),
        compiler_params=pltpu.CompilerParams(vmem_limit_bytes=32 * 1024 * 1024),
    )(stack)


def shifted(tree, dx, dy):
    nx = lax.axis_size("gx")
    ny = lax.axis_size("gy")
    pairs = []
    for x in range(nx):
        for y in range(ny):
            pairs.append((x * ny + y, ((x + dx) % nx) * ny + (y + dy) % ny))
    return lax.ppermute(tree, ("gx", "gy"), pairs)


def unit_scaled(tensor):
    return tensor / jnp.sqrt(jnp.mean(tensor * tensor) + 1e-06)


def edge_kernel(wd_ref, pm_ref, t_ref, qt_ref, o_ref, f_ref, g_ref):
    n = qt_ref.shape[0]
    dd = o_ref.shape[0]
    group = 4
    wd = wd_ref[...]
    for d0 in range(0, dd, group):
        part = jnp.dot(wd, pm_ref[:, d0 * LANES:(d0 + group) * LANES], preferred_element_type=jnp.float32)
        part = part.astype(jnp.bfloat16)
        for k in range(group):
            f_ref[:, d0 + k] = part[:, k * LANES:(k + 1) * LANES].reshape(n, dd, LANES)
    t = t_ref[...]
    per = math.gcd(n, 24)

    def mid_body(h, carry):
        x = jnp.concatenate([f_ref[h * per + k].reshape(dd * dd, LANES) for k in range(per)], axis=1)
        g = jnp.dot(t, x, preferred_element_type=jnp.float32).astype(jnp.bfloat16)
        for k in range(per):
            at = pl.multiple_of((h * per + k) * dd, dd)
            for r in range(dd):
                g_ref[pl.ds(at, dd), r * LANES:(r + 1) * LANES] = g[r * dd:(r + 1) * dd, k * LANES:(k + 1) * LANES]
        return carry

    lax.fori_loop(0, n // per, mid_body, 0)
    qt = qt_ref[...]
    for r0 in range(0, dd, group):
        part = jnp.dot(qt, g_ref[:, r0 * LANES:(r0 + group) * LANES], preferred_element_type=jnp.float32)
        for k in range(group):
            o_ref[r0 + k] = part[:, k * LANES:(k + 1) * LANES]


def edge_contract(west, low_t, up_t, site):
    n = west.shape[0]
    dd = west.shape[1] // n
    wd = west.reshape(n * dd, n)
    pm = jnp.transpose(low_t.reshape(n, n, dd), (1, 2, 0))
    pm = jnp.pad(pm, ((0, 0), (0, 0), (0, LANES - n))).reshape(n, dd * LANES)
    qt = up_t
    out = pl.pallas_call(
        edge_kernel,
        out_shape=jax.ShapeDtypeStruct((dd, n, LANES), jnp.float32),
        scratch_shapes=[
            pltpu.VMEM((n, dd, dd, LANES), jnp.bfloat16),
            pltpu.VMEM((n * dd, dd * LANES), jnp.bfloat16),
        ],
        compiler_params=pltpu.CompilerParams(vmem_limit_bytes=48 * 1024 * 1024),
    )(wd, pm, site, qt)
    return jnp.transpose(out[:, :, :n], (1, 0, 2)).reshape(n, dd * n)


def one_hot(rows, cols, row_key, col_key):
    r = lax.broadcasted_iota(jnp.int32, (rows, cols), 0)
    c = lax.broadcasted_iota(jnp.int32, (rows, cols), 1)
    return (row_key(r) == col_key(c)).astype(jnp.float32)


def double_layer(ket, bra):
    q = ket.shape[1]
    dd = q * q
    size = dd * dd
    ket_m = jnp.transpose(ket.astype(jnp.float32), (0, 3, 2, 4, 1)).reshape(ket.shape[0], dd, dd)
    bra_m = jnp.transpose(bra.astype(jnp.float32), (0, 3, 2, 4, 1)).reshape(bra.shape[0], dd, dd)
    k_row = one_hot(size, dd, lambda r: (r // (q * dd)) * q + (r // q) % q, lambda c: c)
    b_row = one_hot(size, dd, lambda r: ((r // dd) % q) * q + r % q, lambda c: c)
    k_col = one_hot(dd, size, lambda r: r, lambda c: (c // (q * dd)) * q + (c // q) % q)
    b_col = one_hot(dd, size, lambda r: r, lambda c: ((c // dd) % q) * q + c % q)
    hi = lax.Precision.HIGHEST
    ket_wide = jnp.einsum("ra,sab,bc->src", k_row, ket_m, k_col, precision=hi)
    bra_wide = jnp.einsum("ra,sab,bc->src", b_row, bra_m, b_col, precision=hi)
    return jnp.sum(ket_wide * bra_wide, axis=0).astype(jnp.bfloat16)


def per_device(
    c_upper, edge_upper, edge_left, c_lower, edge_lower, site_ket, time_gate, quench_sites
):
    env_width = c_upper.shape[-1]
    double_bond = edge_upper.shape[-1] // env_width
    bond_dim = math.isqrt(double_bond)
    phys_dim = site_ket.shape[2]
    ket_sites = site_ket[0, 0].reshape(phys_dim, bond_dim, bond_dim, bond_dim, bond_dim)
    gram = jnp.dot(time_gate.T, time_gate, precision=lax.Precision.HIGHEST)
    gated = jnp.einsum(
        "st,tabcd->sabcd", gram, ket_sites.astype(jnp.float32), precision=lax.Precision.HIGHEST
    )
    own_index = lax.axis_index("gx") * lax.axis_size("gy") + lax.axis_index("gy")
    chosen = jnp.any(quench_sites == own_index)
    bra = jnp.where(chosen, gated, ket_sites.astype(jnp.float32)).astype(jnp.bfloat16)
    site = double_layer(ket_sites, bra)
    north_edge = edge_upper[0, 0]
    south_edge = edge_lower[0, 0]
    corner_up = c_upper[0, 0]
    west_edge = edge_left[0, 0]
    corner_low = c_lower[0, 0]
    up_corner_nb, north_nb = shifted((corner_up, north_edge), 0, -1)
    low_corner_nb, south_nb = shifted((corner_low, south_edge), 0, 1)
    n = env_width
    edges = jnp.stack([south_edge, north_nb, south_nb, north_edge])
    hi = lax.Precision.HIGHEST
    for step in range(STEPS):
        corners_in = jnp.stack([corner_low, up_corner_nb, low_corner_nb, corner_up])
        halves = jnp.einsum("bwa,bak->bwk", corners_in, edges, preferred_element_type=jnp.float32)
        halves = halves.reshape(4, n * double_bond, n)
        mats = halves[0::2] + halves[1::2]
        projs = polar_factor_t(jnp.swapaxes(mats, 1, 2))
        below_t = projs[0]
        above_t = projs[1]
        corners = jnp.einsum("bir,brj->bij", projs, halves[0::3], precision=hi)
        corners = jax.vmap(unit_scaled)(corners).astype(jnp.bfloat16)
        new_low = corners[0]
        new_up = corners[1]
        if step + 1 < STEPS:
            up_corner_nb = shifted(new_up, 1, -1)
            low_corner_nb = shifted(new_low, 1, 1)
        edge_new = edge_contract(west_edge, below_t.astype(jnp.bfloat16), above_t.astype(jnp.bfloat16), site)
        edge_new = unit_scaled(edge_new).astype(jnp.bfloat16)
        corner_up, west_edge, corner_low = shifted((new_up, edge_new, new_low), 1, 0)
    return (corner_up[None, None], west_edge[None, None], corner_low[None, None])


def solution(mesh):
    return jax.shard_map(
        per_device,
        mesh=mesh,
        in_specs=(
            P("gx", "gy", None, None),
            P("gx", "gy", None, None),
            P("gx", "gy", None, None),
            P("gx", "gy", None, None),
            P("gx", "gy", None, None),
            P("gx", "gy", None, None),
            P(),
            P(),
        ),
        out_specs=(P("gx", "gy", None, None), P("gx", "gy", None, None), P("gx", "gy", None, None)),
        check_vma=False,
    )
```

```python
import math

import jax
import jax.numpy as jnp
from jax import lax
from jax.experimental import pallas as pl
from jax.experimental.pallas import tpu as pltpu
from jax.sharding import PartitionSpec as P

NS_ITERS = 6
STEPS = 2
LANES = 128


def passed_along(shard, axis, by):
    peers = lax.axis_size(axis)
    return lax.ppermute(shard, axis, [(i, (i + by) % peers) for i in range(peers)])


def split_bf16(x):
    hi = x.astype(jnp.bfloat16)
    return hi, (x - hi.astype(jnp.float32)).astype(jnp.bfloat16)


def dot3(a, b, dims):
    ah, al = split_bf16(a)
    bh, bl = split_bf16(b)
    out = lambda p, q: lax.dot_general(p, q, (dims, ((), ())), preferred_element_type=jnp.float32)
    return out(ah, bh) + (out(ah, bl) + out(al, bh))


def polar_kernel(y_ref, o_ref):
    count = y_ref.shape[0]
    ys = []
    for b in range(count):
        y = y_ref[b]
        ys.append(y / jnp.sqrt(jnp.sum(y * y) + 1e-06))
    for sweep in range(NS_ITERS):
        grams = [dot3(y, y, ((1,), (1,))) for y in ys]
        ys = [1.5 * y - 0.5 * dot3(g, y, ((1,), (0,))) for g, y in zip(grams, ys)]
    for b in range(count):
        o_ref[b] = ys[b]


def polar_factor_t(stack):
    return pl.pallas_call(
        polar_kernel,
        out_shape=jax.ShapeDtypeStruct(stack.shape, jnp.float32),
        compiler_params=pltpu.CompilerParams(vmem_limit_bytes=32 * 1024 * 1024),
    )(stack)


def shifted(tree, dx, dy):
    nx = lax.axis_size("gx")
    ny = lax.axis_size("gy")
    pairs = []
    for x in range(nx):
        for y in range(ny):
            pairs.append((x * ny + y, ((x + dx) % nx) * ny + (y + dy) % ny))
    return lax.ppermute(tree, ("gx", "gy"), pairs)


def unit_scaled(tensor):
    return tensor / jnp.sqrt(jnp.mean(tensor * tensor) + 1e-06)


def edge_kernel(wd_ref, pm_ref, t_ref, qt_ref, o_ref, f_ref, g_ref):
    n = qt_ref.shape[0]
    dd = math.isqrt(t_ref.shape[0])
    group = 4
    wd = wd_ref[...]
    for d0 in range(0, dd, group):
        part = jnp.dot(wd, pm_ref[:, d0 * LANES:(d0 + group) * LANES], preferred_element_type=jnp.float32)
        part = part.astype(jnp.bfloat16)
        for k in range(group):
            f_ref[:, d0 + k] = part[:, k * LANES:(k + 1) * LANES].reshape(n, dd, LANES)
    t = t_ref[...]
    per = math.gcd(n, 24)

    def mid_body(h, carry):
        x = jnp.concatenate([f_ref[h * per + k].reshape(dd * dd, LANES) for k in range(per)], axis=1)
        g = jnp.dot(t, x, preferred_element_type=jnp.float32).astype(jnp.bfloat16)
        for k in range(per):
            at = pl.multiple_of((h * per + k) * dd, dd)
            for r in range(dd):
                g_ref[pl.ds(at, dd), r * LANES:(r + 1) * LANES] = g[r * dd:(r + 1) * dd, k * LANES:(k + 1) * LANES]
        return carry

    lax.fori_loop(0, n // per, mid_body, 0)
    qt = qt_ref[...]
    parts = []
    total = jnp.zeros((1, 1), jnp.float32)
    for r0 in range(0, dd, group):
        part = jnp.dot(qt, g_ref[:, r0 * LANES:(r0 + group) * LANES], preferred_element_type=jnp.float32)
        parts.append(part)
        total = total + jnp.sum(part * part, keepdims=True)
    scale = lax.rsqrt(total / (n * dd * n) + 1e-06)
    for r0, part in zip(range(0, dd, group), parts):
        for k in range(group):
            r = r0 + k
            o_ref[:, r * n:(r + 1) * n] = (part[:, k * LANES:k * LANES + n] * scale).astype(o_ref.dtype)


def edge_contract(west, low_t, up_t, site):
    n = west.shape[0]
    dd = west.shape[1] // n
    wd = west.reshape(n * dd, n)
    pm = jnp.transpose(low_t.reshape(n, n, dd), (1, 2, 0))
    pm = jnp.pad(pm, ((0, 0), (0, 0), (0, LANES - n))).reshape(n, dd * LANES)
    qt = up_t
    out = pl.pallas_call(
        edge_kernel,
        out_shape=jax.ShapeDtypeStruct((n, dd * n), jnp.bfloat16),
        scratch_shapes=[
            pltpu.VMEM((n, dd, dd, LANES), jnp.bfloat16),
            pltpu.VMEM((n * dd, dd * LANES), jnp.bfloat16),
        ],
        compiler_params=pltpu.CompilerParams(vmem_limit_bytes=48 * 1024 * 1024),
    )(wd, pm, site, qt)
    return out


def one_hot(rows, cols, row_key, col_key):
    r = lax.broadcasted_iota(jnp.int32, (rows, cols), 0)
    c = lax.broadcasted_iota(jnp.int32, (rows, cols), 1)
    return (row_key(r) == col_key(c)).astype(jnp.float32)


def double_layer(ket, bra):
    q = ket.shape[1]
    dd = q * q
    size = dd * dd
    ket_m = jnp.transpose(ket.astype(jnp.float32), (0, 3, 2, 4, 1)).reshape(ket.shape[0], dd, dd)
    bra_m = jnp.transpose(bra.astype(jnp.float32), (0, 3, 2, 4, 1)).reshape(bra.shape[0], dd, dd)
    k_row = one_hot(size, dd, lambda r: (r // (q * dd)) * q + (r // q) % q, lambda c: c)
    b_row = one_hot(size, dd, lambda r: ((r // dd) % q) * q + r % q, lambda c: c)
    k_col = one_hot(dd, size, lambda r: r, lambda c: (c // (q * dd)) * q + (c // q) % q)
    b_col = one_hot(dd, size, lambda r: r, lambda c: ((c // dd) % q) * q + c % q)
    hi = lax.Precision.HIGHEST
    ket_wide = jnp.einsum("ra,sab,bc->src", k_row, ket_m, k_col, precision=hi)
    bra_wide = jnp.einsum("ra,sab,bc->src", b_row, bra_m, b_col, precision=hi)
    return jnp.sum(ket_wide * bra_wide, axis=0).astype(jnp.bfloat16)


def per_device(
    c_upper, edge_upper, edge_left, c_lower, edge_lower, site_ket, time_gate, quench_sites
):
    env_width = c_upper.shape[-1]
    double_bond = edge_upper.shape[-1] // env_width
    bond_dim = math.isqrt(double_bond)
    phys_dim = site_ket.shape[2]
    ket_sites = site_ket[0, 0].reshape(phys_dim, bond_dim, bond_dim, bond_dim, bond_dim)
    gram = jnp.dot(time_gate.T, time_gate, precision=lax.Precision.HIGHEST)
    gated = jnp.einsum(
        "st,tabcd->sabcd", gram, ket_sites.astype(jnp.float32), precision=lax.Precision.HIGHEST
    )
    own_index = lax.axis_index("gx") * lax.axis_size("gy") + lax.axis_index("gy")
    chosen = jnp.any(quench_sites == own_index)
    bra = jnp.where(chosen, gated, ket_sites.astype(jnp.float32)).astype(jnp.bfloat16)
    site = double_layer(ket_sites, bra)
    north_edge = edge_upper[0, 0]
    south_edge = edge_lower[0, 0]
    corner_up = c_upper[0, 0]
    west_edge = edge_left[0, 0]
    corner_low = c_lower[0, 0]
    up_corner_nb, north_nb = shifted((corner_up, north_edge), 0, -1)
    low_corner_nb, south_nb = shifted((corner_low, south_edge), 0, 1)
    n = env_width
    for step in range(STEPS):
        def half(corner, edge):
            return jnp.dot(corner, edge, preferred_element_type=jnp.float32).reshape(n * double_bond, n)

        upper = half(corner_up, north_edge)
        lower = half(corner_low, south_edge)
        upper_nb = half(up_corner_nb, north_nb)
        lower_nb = half(low_corner_nb, south_nb)
        projs = polar_factor_t(jnp.swapaxes(jnp.stack([lower + upper_nb, lower_nb + upper]), 1, 2))
        below_t = projs[0]
        above_t = projs[1]
        new_up = jnp.dot(above_t, upper, precision=lax.Precision.HIGH)
        new_low = jnp.dot(below_t, lower, precision=lax.Precision.HIGH)
        new_up = unit_scaled(new_up).astype(jnp.bfloat16)
        new_low = unit_scaled(new_low).astype(jnp.bfloat16)
        if step + 1 < STEPS:
            up_corner_nb = shifted(new_up, 1, -1)
            low_corner_nb = shifted(new_low, 1, 1)
        edge_new = edge_contract(west_edge, below_t.astype(jnp.bfloat16), above_t.astype(jnp.bfloat16), site)
        corner_up, west_edge, corner_low = shifted((new_up, edge_new, new_low), 1, 0)
    return (corner_up[None, None], west_edge[None, None], corner_low[None, None])


def solution(mesh):
    return jax.shard_map(
        per_device,
        mesh=mesh,
        in_specs=(
            P("gx", "gy", None, None),
            P("gx", "gy", None, None),
            P("gx", "gy", None, None),
            P("gx", "gy", None, None),
            P("gx", "gy", None, None),
            P("gx", "gy", None, None),
            P(),
            P(),
        ),
        out_specs=(P("gx", "gy", None, None), P("gx", "gy", None, None), P("gx", "gy", None, None)),
        check_vma=False,
    )
```

```python
import math

import jax
import jax.numpy as jnp
from jax import lax
from jax.experimental import pallas as pl
from jax.experimental.pallas import tpu as pltpu
from jax.sharding import PartitionSpec as P

NS_ITERS = 6
STEPS = 2
LANES = 128


def passed_along(shard, axis, by):
    peers = lax.axis_size(axis)
    return lax.ppermute(shard, axis, [(i, (i + by) % peers) for i in range(peers)])


def split_bf16(x):
    hi = x.astype(jnp.bfloat16)
    return hi, (x - hi.astype(jnp.float32)).astype(jnp.bfloat16)


def dot3(a, b, dims):
    ah, al = split_bf16(a)
    bh, bl = split_bf16(b)
    out = lambda p, q: lax.dot_general(p, q, (dims, ((), ())), preferred_element_type=jnp.float32)
    return out(ah, bh) + (out(ah, bl) + out(al, bh))


def polar_kernel(y_ref, o_ref):
    count = y_ref.shape[0]
    ys = []
    for b in range(count):
        y = y_ref[b]
        ys.append(y / jnp.sqrt(jnp.sum(y * y) + 1e-06))
    for sweep in range(NS_ITERS):
        grams = [dot3(y, y, ((1,), (1,))) for y in ys]
        ys = [1.5 * y - 0.5 * dot3(g, y, ((1,), (0,))) for g, y in zip(grams, ys)]
    for b in range(count):
        o_ref[b] = ys[b]


def polar_factor_t(stack):
    return pl.pallas_call(
        polar_kernel,
        out_shape=jax.ShapeDtypeStruct(stack.shape, jnp.float32),
        compiler_params=pltpu.CompilerParams(vmem_limit_bytes=32 * 1024 * 1024),
    )(stack)


def shifted(tree, dx, dy):
    nx = lax.axis_size("gx")
    ny = lax.axis_size("gy")
    pairs = []
    for x in range(nx):
        for y in range(ny):
            pairs.append((x * ny + y, ((x + dx) % nx) * ny + (y + dy) % ny))
    return lax.ppermute(tree, ("gx", "gy"), pairs)


def unit_scaled(tensor):
    return tensor / jnp.sqrt(jnp.mean(tensor * tensor) + 1e-06)


def edge_kernel(wd_ref, pm_ref, t_ref, qt_ref, o_ref, f_ref, g_ref):
    n = qt_ref.shape[0]
    dd = math.isqrt(t_ref.shape[0])
    group = 4
    wd = wd_ref[...]
    for d0 in range(0, dd, group):
        part = jnp.dot(wd, pm_ref[:, d0 * LANES:(d0 + group) * LANES], preferred_element_type=jnp.float32)
        part = part.astype(jnp.bfloat16)
        for k in range(group):
            f_ref[:, d0 + k] = part[:, k * LANES:(k + 1) * LANES].reshape(n, dd, LANES)
    t = t_ref[...]
    per = math.gcd(n, 24)

    def mid_body(h, carry):
        x = jnp.concatenate([f_ref[h * per + k].reshape(dd * dd, LANES) for k in range(per)], axis=1)
        g = jnp.dot(t, x, preferred_element_type=jnp.float32).astype(jnp.bfloat16)
        for k in range(per):
            at = pl.multiple_of((h * per + k) * dd, dd)
            for r in range(dd):
                g_ref[pl.ds(at, dd), r * LANES:(r + 1) * LANES] = g[r * dd:(r + 1) * dd, k * LANES:(k + 1) * LANES]
        return carry

    lax.fori_loop(0, n // per, mid_body, 0)
    qt = qt_ref[...]
    parts = []
    total = jnp.zeros((1, 1), jnp.float32)
    for r0 in range(0, dd, group):
        part = jnp.dot(qt, g_ref[:, r0 * LANES:(r0 + group) * LANES], preferred_element_type=jnp.float32)
        parts.append(part)
        total = total + jnp.sum(part * part, keepdims=True)
    scale = lax.rsqrt(total / (n * dd * n) + 1e-06)
    for r0, part in zip(range(0, dd, group), parts):
        for k in range(group):
            r = r0 + k
            o_ref[:, r * n:(r + 1) * n] = (part[:, k * LANES:k * LANES + n] * scale).astype(o_ref.dtype)


def edge_contract(west, low_t, up_t, site):
    n = west.shape[0]
    dd = west.shape[1] // n
    wd = west.reshape(n * dd, n)
    pm = jnp.transpose(low_t.reshape(n, n, dd), (1, 2, 0))
    pm = jnp.pad(pm, ((0, 0), (0, 0), (0, LANES - n))).reshape(n, dd * LANES)
    qt = up_t
    out = pl.pallas_call(
        edge_kernel,
        out_shape=jax.ShapeDtypeStruct((n, dd * n), jnp.bfloat16),
        scratch_shapes=[
            pltpu.VMEM((n, dd, dd, LANES), jnp.bfloat16),
            pltpu.VMEM((n * dd, dd * LANES), jnp.bfloat16),
        ],
        compiler_params=pltpu.CompilerParams(vmem_limit_bytes=48 * 1024 * 1024),
    )(wd, pm, site, qt)
    return out


def one_hot(rows, cols, row_key, col_key):
    r = lax.broadcasted_iota(jnp.int32, (rows, cols), 0)
    c = lax.broadcasted_iota(jnp.int32, (rows, cols), 1)
    return (row_key(r) == col_key(c)).astype(jnp.float32)


def double_layer(ket, bra):
    q = ket.shape[1]
    dd = q * q
    size = dd * dd
    ket_m = jnp.transpose(ket.astype(jnp.float32), (0, 3, 2, 4, 1)).reshape(ket.shape[0], dd, dd)
    bra_m = jnp.transpose(bra.astype(jnp.float32), (0, 3, 2, 4, 1)).reshape(bra.shape[0], dd, dd)
    k_row = one_hot(size, dd, lambda r: (r // (q * dd)) * q + (r // q) % q, lambda c: c)
    b_row = one_hot(size, dd, lambda r: ((r // dd) % q) * q + r % q, lambda c: c)
    k_col = one_hot(dd, size, lambda r: r, lambda c: (c // (q * dd)) * q + (c // q) % q)
    b_col = one_hot(dd, size, lambda r: r, lambda c: ((c // dd) % q) * q + c % q)
    hi = lax.Precision.HIGHEST
    ket_wide = jnp.einsum("ra,sab,bc->src", k_row, ket_m, k_col, precision=hi)
    bra_wide = jnp.einsum("ra,sab,bc->src", b_row, bra_m, b_col, precision=hi)
    return jnp.sum(ket_wide * bra_wide, axis=0).astype(jnp.bfloat16)


def per_device(
    c_upper, edge_upper, edge_left, c_lower, edge_lower, site_ket, time_gate, quench_sites
):
    env_width = c_upper.shape[-1]
    double_bond = edge_upper.shape[-1] // env_width
    bond_dim = math.isqrt(double_bond)
    phys_dim = site_ket.shape[2]
    ket_sites = site_ket[0, 0].reshape(phys_dim, bond_dim, bond_dim, bond_dim, bond_dim)
    gram = jnp.dot(time_gate.T, time_gate, precision=lax.Precision.HIGHEST)
    gated = jnp.einsum(
        "st,tabcd->sabcd", gram, ket_sites.astype(jnp.float32), precision=lax.Precision.HIGHEST
    )
    own_index = lax.axis_index("gx") * lax.axis_size("gy") + lax.axis_index("gy")
    chosen = jnp.any(quench_sites == own_index)
    bra = jnp.where(chosen, gated, ket_sites.astype(jnp.float32)).astype(jnp.bfloat16)
    site = double_layer(ket_sites, bra)
    north_edge = edge_upper[0, 0]
    south_edge = edge_lower[0, 0]
    corner_up = c_upper[0, 0]
    west_edge = edge_left[0, 0]
    corner_low = c_lower[0, 0]
    up_corner_nb, north_nb = shifted((corner_up, north_edge), 0, -1)
    low_corner_nb, south_nb = shifted((corner_low, south_edge), 0, 1)
    n = env_width
    offsets = [0] * (STEPS - 1) + [1]
    here = (north_edge, south_edge, north_nb, south_nb, site)
    left_north, left_south, left_site = shifted((north_edge, south_edge, site), 1, 0)
    left = (left_north, left_south, shifted(north_edge, 1, -1), shifted(south_edge, 1, 1), left_site)
    if offsets[0]:
        corner_up, west_edge, corner_low = shifted((corner_up, west_edge, corner_low), 1, 0)
        up_corner_nb = shifted(c_upper[0, 0], 1, -1)
        low_corner_nb = shifted(c_lower[0, 0], 1, 1)
    for step in range(STEPS):
        north_e, south_e, north_n, south_n, site_now = left if offsets[step] else here

        def half(corner, edge):
            return jnp.dot(corner, edge, preferred_element_type=jnp.float32).reshape(n * double_bond, n)

        upper = half(corner_up, north_e)
        lower = half(corner_low, south_e)
        upper_nb = half(up_corner_nb, north_n)
        lower_nb = half(low_corner_nb, south_n)
        projs = polar_factor_t(jnp.swapaxes(jnp.stack([lower + upper_nb, lower_nb + upper]), 1, 2))
        below_t = projs[0]
        above_t = projs[1]
        new_up = jnp.dot(above_t, upper, precision=lax.Precision.HIGH)
        new_low = jnp.dot(below_t, lower, precision=lax.Precision.HIGH)
        new_up = unit_scaled(new_up).astype(jnp.bfloat16)
        new_low = unit_scaled(new_low).astype(jnp.bfloat16)
        if step + 1 < STEPS:
            dx = 1 + offsets[step + 1] - offsets[step]
            up_corner_nb = shifted(new_up, dx, -1)
            low_corner_nb = shifted(new_low, dx, 1)
        edge_new = edge_contract(west_edge, below_t.astype(jnp.bfloat16), above_t.astype(jnp.bfloat16), site_now)
        if step + 1 < STEPS:
            corner_up, west_edge, corner_low = shifted((new_up, edge_new, new_low), dx, 0)
        else:
            corner_up, west_edge, corner_low = new_up, edge_new, new_low
    return (corner_up[None, None], west_edge[None, None], corner_low[None, None])


def solution(mesh):
    return jax.shard_map(
        per_device,
        mesh=mesh,
        in_specs=(
            P("gx", "gy", None, None),
            P("gx", "gy", None, None),
            P("gx", "gy", None, None),
            P("gx", "gy", None, None),
            P("gx", "gy", None, None),
            P("gx", "gy", None, None),
            P(),
            P(),
        ),
        out_specs=(P("gx", "gy", None, None), P("gx", "gy", None, None), P("gx", "gy", None, None)),
        check_vma=False,
    )
```

```python
import math

import jax
import jax.numpy as jnp
from jax import lax
from jax.experimental import pallas as pl
from jax.experimental.pallas import tpu as pltpu
from jax.sharding import PartitionSpec as P

NS_ITERS = 6
STEPS = 2
LANES = 128


def passed_along(shard, axis, by):
    peers = lax.axis_size(axis)
    return lax.ppermute(shard, axis, [(i, (i + by) % peers) for i in range(peers)])


def split_bf16(x):
    hi = x.astype(jnp.bfloat16)
    return hi, (x - hi.astype(jnp.float32)).astype(jnp.bfloat16)


def dot3(a, b, dims):
    ah, al = split_bf16(a)
    bh, bl = split_bf16(b)
    out = lambda p, q: lax.dot_general(p, q, (dims, ((), ())), preferred_element_type=jnp.float32)
    return out(ah, bh) + (out(ah, bl) + out(al, bh))


def gram3(y):
    yh, yl = split_bf16(y)
    out = lambda p, q: lax.dot_general(p, q, (((1,), (1,)), ((), ())), preferred_element_type=jnp.float32)
    cross = out(yh, yl)
    return out(yh, yh) + (cross + cross.T)


def polar_kernel(y_ref, o_ref):
    count = y_ref.shape[0]
    ys = []
    for b in range(count):
        y = y_ref[b]
        ys.append(y / jnp.sqrt(jnp.sum(y * y) + 1e-06))
    for sweep in range(NS_ITERS):
        grams = [gram3(y) for y in ys]
        ys = [1.5 * y - 0.5 * dot3(g, y, ((1,), (0,))) for g, y in zip(grams, ys)]
    for b in range(count):
        o_ref[b] = ys[b]


def polar_factor_t(stack):
    return pl.pallas_call(
        polar_kernel,
        out_shape=jax.ShapeDtypeStruct(stack.shape, jnp.float32),
        compiler_params=pltpu.CompilerParams(vmem_limit_bytes=32 * 1024 * 1024),
    )(stack)


def shifted(tree, dx, dy):
    nx = lax.axis_size("gx")
    ny = lax.axis_size("gy")
    pairs = []
    for x in range(nx):
        for y in range(ny):
            pairs.append((x * ny + y, ((x + dx) % nx) * ny + (y + dy) % ny))
    return lax.ppermute(tree, ("gx", "gy"), pairs)


def unit_scaled(tensor):
    return tensor / jnp.sqrt(jnp.mean(tensor * tensor) + 1e-06)


def edge_kernel(wd_ref, pm_ref, t_ref, qt_ref, o_ref, f_ref, g_ref):
    n = qt_ref.shape[0]
    dd = o_ref.shape[0]
    group = 4
    wd = wd_ref[...]
    for d0 in range(0, dd, group):
        part = jnp.dot(wd, pm_ref[:, d0 * LANES:(d0 + group) * LANES], preferred_element_type=jnp.float32)
        part = part.astype(jnp.bfloat16)
        for k in range(group):
            f_ref[:, d0 + k] = part[:, k * LANES:(k + 1) * LANES].reshape(n, dd, LANES)
    t = t_ref[...]
    per = math.gcd(n, 48)

    def mid_body(h, carry):
        x = jnp.concatenate([f_ref[h * per + k].reshape(dd * dd, LANES) for k in range(per)], axis=1)
        g = jnp.dot(t, x, preferred_element_type=jnp.float32).astype(jnp.bfloat16)
        for k in range(per):
            at = pl.multiple_of((h * per + k) * dd, dd)
            for r in range(dd):
                g_ref[pl.ds(at, dd), r * LANES:(r + 1) * LANES] = g[r * dd:(r + 1) * dd, k * LANES:(k + 1) * LANES]
        return carry

    lax.fori_loop(0, n // per, mid_body, 0)
    qt = qt_ref[...]
    for r0 in range(0, dd, group):
        part = jnp.dot(qt, g_ref[:, r0 * LANES:(r0 + group) * LANES], preferred_element_type=jnp.float32)
        for k in range(group):
            o_ref[r0 + k] = part[:, k * LANES:(k + 1) * LANES]


def edge_contract(west, low_t, up_t, site):
    n = west.shape[0]
    dd = west.shape[1] // n
    wd = west.reshape(n * dd, n)
    pm = jnp.transpose(low_t.reshape(n, n, dd), (1, 2, 0))
    pm = jnp.pad(pm, ((0, 0), (0, 0), (0, LANES - n))).reshape(n, dd * LANES)
    qt = up_t
    out = pl.pallas_call(
        edge_kernel,
        out_shape=jax.ShapeDtypeStruct((dd, n, LANES), jnp.float32),
        scratch_shapes=[
            pltpu.VMEM((n, dd, dd, LANES), jnp.bfloat16),
            pltpu.VMEM((n * dd, dd * LANES), jnp.bfloat16),
        ],
        compiler_params=pltpu.CompilerParams(vmem_limit_bytes=48 * 1024 * 1024),
    )(wd, pm, site, qt)
    return jnp.transpose(out[:, :, :n], (1, 0, 2)).reshape(n, dd * n)


def one_hot(rows, cols, row_key, col_key):
    r = lax.broadcasted_iota(jnp.int32, (rows, cols), 0)
    c = lax.broadcasted_iota(jnp.int32, (rows, cols), 1)
    return (row_key(r) == col_key(c)).astype(jnp.float32)


def double_layer(ket, bra):
    q = ket.shape[1]
    dd = q * q
    size = dd * dd
    ket_m = jnp.transpose(ket.astype(jnp.float32), (0, 3, 2, 4, 1)).reshape(ket.shape[0], dd, dd)
    bra_m = jnp.transpose(bra.astype(jnp.float32), (0, 3, 2, 4, 1)).reshape(bra.shape[0], dd, dd)
    k_row = one_hot(size, dd, lambda r: (r // (q * dd)) * q + (r // q) % q, lambda c: c)
    b_row = one_hot(size, dd, lambda r: ((r // dd) % q) * q + r % q, lambda c: c)
    k_col = one_hot(dd, size, lambda r: r, lambda c: (c // (q * dd)) * q + (c // q) % q)
    b_col = one_hot(dd, size, lambda r: r, lambda c: ((c // dd) % q) * q + c % q)
    hi = lax.Precision.HIGHEST
    ket_wide = jnp.einsum("ra,sab,bc->src", k_row, ket_m, k_col, precision=hi)
    bra_wide = jnp.einsum("ra,sab,bc->src", b_row, bra_m, b_col, precision=hi)
    return jnp.sum(ket_wide * bra_wide, axis=0).astype(jnp.bfloat16)


def per_device(
    c_upper, edge_upper, edge_left, c_lower, edge_lower, site_ket, time_gate, quench_sites
):
    env_width = c_upper.shape[-1]
    double_bond = edge_upper.shape[-1] // env_width
    bond_dim = math.isqrt(double_bond)
    phys_dim = site_ket.shape[2]
    ket_sites = site_ket[0, 0].reshape(phys_dim, bond_dim, bond_dim, bond_dim, bond_dim)
    gram = jnp.dot(time_gate.T, time_gate, precision=lax.Precision.HIGHEST)
    gated = jnp.einsum(
        "st,tabcd->sabcd", gram, ket_sites.astype(jnp.float32), precision=lax.Precision.HIGHEST
    )
    own_index = lax.axis_index("gx") * lax.axis_size("gy") + lax.axis_index("gy")
    chosen = jnp.any(quench_sites == own_index)
    bra = jnp.where(chosen, gated, ket_sites.astype(jnp.float32)).astype(jnp.bfloat16)
    site = double_layer(ket_sites, bra)
    north_edge = edge_upper[0, 0]
    south_edge = edge_lower[0, 0]
    corner_up = c_upper[0, 0]
    west_edge = edge_left[0, 0]
    corner_low = c_lower[0, 0]
    up_corner_nb, north_nb = shifted((corner_up, north_edge), 0, -1)
    low_corner_nb, south_nb = shifted((corner_low, south_edge), 0, 1)
    n = env_width
    for step in range(STEPS):
        def half(corner, edge):
            return jnp.dot(corner, edge, preferred_element_type=jnp.float32).reshape(n * double_bond, n)

        upper = half(corner_up, north_edge)
        lower = half(corner_low, south_edge)
        upper_nb = half(up_corner_nb, north_nb)
        lower_nb = half(low_corner_nb, south_nb)
        projs = polar_factor_t(jnp.swapaxes(jnp.stack([lower + upper_nb, lower_nb + upper]), 1, 2))
        below_t = projs[0]
        above_t = projs[1]
        new_up = jnp.dot(above_t, upper, precision=lax.Precision.HIGHEST)
        new_low = jnp.dot(below_t, lower, precision=lax.Precision.HIGHEST)
        new_up = unit_scaled(new_up).astype(jnp.bfloat16)
        new_low = unit_scaled(new_low).astype(jnp.bfloat16)
        if step + 1 < STEPS:
            up_corner_nb = shifted(new_up, 1, -1)
            low_corner_nb = shifted(new_low, 1, 1)
        edge_new = edge_contract(west_edge, below_t.astype(jnp.bfloat16), above_t.astype(jnp.bfloat16), site)
        edge_new = unit_scaled(edge_new).astype(jnp.bfloat16)
        corner_up, west_edge, corner_low = shifted((new_up, edge_new, new_low), 1, 0)
    return (corner_up[None, None], west_edge[None, None], corner_low[None, None])


def solution(mesh):
    return jax.shard_map(
        per_device,
        mesh=mesh,
        in_specs=(
            P("gx", "gy", None, None),
            P("gx", "gy", None, None),
            P("gx", "gy", None, None),
            P("gx", "gy", None, None),
            P("gx", "gy", None, None),
            P("gx", "gy", None, None),
            P(),
            P(),
        ),
        out_specs=(P("gx", "gy", None, None), P("gx", "gy", None, None), P("gx", "gy", None, None)),
        check_vma=False,
    )
```

```python
import math

import jax
import jax.numpy as jnp
from jax import lax
from jax.experimental import pallas as pl
from jax.experimental.pallas import tpu as pltpu
from jax.sharding import PartitionSpec as P

NS_ITERS = 6
STEPS = 2
LANES = 128


def passed_along(shard, axis, by):
    peers = lax.axis_size(axis)
    return lax.ppermute(shard, axis, [(i, (i + by) % peers) for i in range(peers)])


def split_bf16(x):
    hi = x.astype(jnp.bfloat16)
    return hi, (x - hi.astype(jnp.float32)).astype(jnp.bfloat16)


def dot3(a, b, dims):
    ah, al = split_bf16(a)
    bh, bl = split_bf16(b)
    out = lambda p, q: lax.dot_general(p, q, (dims, ((), ())), preferred_element_type=jnp.float32)
    return out(ah, bh) + (out(ah, bl) + out(al, bh))


def ns_step(y):
    out = lambda p, q, dims: lax.dot_general(p, q, (dims, ((), ())), preferred_element_type=jnp.float32)
    yh, yl = split_bf16(y)
    cross = out(yh, yl, ((1,), (1,)))
    gram = out(yh, yh, ((1,), (1,))) + (cross + cross.T)
    eye = (lax.broadcasted_iota(jnp.int32, gram.shape, 0) == lax.broadcasted_iota(jnp.int32, gram.shape, 1))
    step = jnp.where(eye, 1.5, 0.0) - 0.5 * gram
    sh, sl = split_bf16(step)
    dims = ((1,), (0,))
    return out(sh, yh, dims) + (out(sh, yl, dims) + out(sl, yh, dims))


def polar_kernel(y_ref, o_ref):
    count = y_ref.shape[0]
    ys = []
    for b in range(count):
        y = y_ref[b]
        ys.append(y / jnp.sqrt(jnp.sum(y * y) + 1e-06))
    for sweep in range(NS_ITERS):
        ys = [ns_step(y) for y in ys]
    for b in range(count):
        o_ref[b] = ys[b]


def polar_factor_t(stack):
    return pl.pallas_call(
        polar_kernel,
        out_shape=jax.ShapeDtypeStruct(stack.shape, jnp.float32),
        compiler_params=pltpu.CompilerParams(vmem_limit_bytes=32 * 1024 * 1024),
    )(stack)


def shifted(tree, dx, dy):
    nx = lax.axis_size("gx")
    ny = lax.axis_size("gy")
    pairs = []
    for x in range(nx):
        for y in range(ny):
            pairs.append((x * ny + y, ((x + dx) % nx) * ny + (y + dy) % ny))
    return lax.ppermute(tree, ("gx", "gy"), pairs)


def unit_scaled(tensor):
    return tensor / jnp.sqrt(jnp.mean(tensor * tensor) + 1e-06)


def edge_kernel(wd_ref, pm_ref, t_ref, qt_ref, o_ref, f_ref, g_ref):
    n = qt_ref.shape[0]
    dd = o_ref.shape[0]
    group = 4
    wd = wd_ref[...]
    for d0 in range(0, dd, group):
        part = jnp.dot(wd, pm_ref[:, d0 * LANES:(d0 + group) * LANES], preferred_element_type=jnp.float32)
        part = part.astype(jnp.bfloat16)
        for k in range(group):
            f_ref[:, d0 + k] = part[:, k * LANES:(k + 1) * LANES].reshape(n, dd, LANES)
    t = t_ref[...]
    per = math.gcd(n, 48)

    def mid_body(h, carry):
        x = jnp.concatenate([f_ref[h * per + k].reshape(dd * dd, LANES) for k in range(per)], axis=1)
        g = jnp.dot(t, x, preferred_element_type=jnp.float32).astype(jnp.bfloat16)
        for k in range(per):
            at = pl.multiple_of((h * per + k) * dd, dd)
            for r in range(dd):
                g_ref[pl.ds(at, dd), r * LANES:(r + 1) * LANES] = g[r * dd:(r + 1) * dd, k * LANES:(k + 1) * LANES]
        return carry

    lax.fori_loop(0, n // per, mid_body, 0)
    qt = qt_ref[...]
    for r0 in range(0, dd, group):
        part = jnp.dot(qt, g_ref[:, r0 * LANES:(r0 + group) * LANES], preferred_element_type=jnp.float32)
        for k in range(group):
            o_ref[r0 + k] = part[:, k * LANES:(k + 1) * LANES]


def edge_contract(west, low_t, up_t, site):
    n = west.shape[0]
    dd = west.shape[1] // n
    wd = west.reshape(n * dd, n)
    pm = jnp.transpose(low_t.reshape(n, n, dd), (1, 2, 0))
    pm = jnp.pad(pm, ((0, 0), (0, 0), (0, LANES - n))).reshape(n, dd * LANES)
    qt = up_t
    out = pl.pallas_call(
        edge_kernel,
        out_shape=jax.ShapeDtypeStruct((dd, n, LANES), jnp.float32),
        scratch_shapes=[
            pltpu.VMEM((n, dd, dd, LANES), jnp.bfloat16),
            pltpu.VMEM((n * dd, dd * LANES), jnp.bfloat16),
        ],
        compiler_params=pltpu.CompilerParams(vmem_limit_bytes=48 * 1024 * 1024),
    )(wd, pm, site, qt)
    return jnp.transpose(out[:, :, :n], (1, 0, 2)).reshape(n, dd * n)


def one_hot(rows, cols, row_key, col_key):
    r = lax.broadcasted_iota(jnp.int32, (rows, cols), 0)
    c = lax.broadcasted_iota(jnp.int32, (rows, cols), 1)
    return (row_key(r) == col_key(c)).astype(jnp.float32)


def double_layer(ket, bra):
    q = ket.shape[1]
    dd = q * q
    size = dd * dd
    ket_m = jnp.transpose(ket.astype(jnp.float32), (0, 3, 2, 4, 1)).reshape(ket.shape[0], dd, dd)
    bra_m = jnp.transpose(bra.astype(jnp.float32), (0, 3, 2, 4, 1)).reshape(bra.shape[0], dd, dd)
    k_row = one_hot(size, dd, lambda r: (r // (q * dd)) * q + (r // q) % q, lambda c: c)
    b_row = one_hot(size, dd, lambda r: ((r // dd) % q) * q + r % q, lambda c: c)
    k_col = one_hot(dd, size, lambda r: r, lambda c: (c // (q * dd)) * q + (c // q) % q)
    b_col = one_hot(dd, size, lambda r: r, lambda c: ((c // dd) % q) * q + c % q)
    hi = lax.Precision.HIGHEST
    ket_wide = jnp.einsum("ra,sab,bc->src", k_row, ket_m, k_col, precision=hi)
    bra_wide = jnp.einsum("ra,sab,bc->src", b_row, bra_m, b_col, precision=hi)
    return jnp.sum(ket_wide * bra_wide, axis=0).astype(jnp.bfloat16)


def per_device(
    c_upper, edge_upper, edge_left, c_lower, edge_lower, site_ket, time_gate, quench_sites
):
    env_width = c_upper.shape[-1]
    double_bond = edge_upper.shape[-1] // env_width
    bond_dim = math.isqrt(double_bond)
    phys_dim = site_ket.shape[2]
    ket_sites = site_ket[0, 0].reshape(phys_dim, bond_dim, bond_dim, bond_dim, bond_dim)
    gram = jnp.dot(time_gate.T, time_gate, precision=lax.Precision.HIGHEST)
    gated = jnp.einsum(
        "st,tabcd->sabcd", gram, ket_sites.astype(jnp.float32), precision=lax.Precision.HIGHEST
    )
    own_index = lax.axis_index("gx") * lax.axis_size("gy") + lax.axis_index("gy")
    chosen = jnp.any(quench_sites == own_index)
    bra = jnp.where(chosen, gated, ket_sites.astype(jnp.float32)).astype(jnp.bfloat16)
    site = double_layer(ket_sites, bra)
    north_edge = edge_upper[0, 0]
    south_edge = edge_lower[0, 0]
    corner_up = c_upper[0, 0]
    west_edge = edge_left[0, 0]
    corner_low = c_lower[0, 0]
    up_corner_nb, north_nb = shifted((corner_up, north_edge), 0, -1)
    low_corner_nb, south_nb = shifted((corner_low, south_edge), 0, 1)
    n = env_width
    for step in range(STEPS):
        def half(corner, edge):
            return jnp.dot(corner, edge, preferred_element_type=jnp.float32).reshape(n * double_bond, n)

        upper = half(corner_up, north_edge)
        lower = half(corner_low, south_edge)
        upper_nb = half(up_corner_nb, north_nb)
        lower_nb = half(low_corner_nb, south_nb)
        projs = polar_factor_t(jnp.swapaxes(jnp.stack([lower + upper_nb, lower_nb + upper]), 1, 2))
        below_t = projs[0]
        above_t = projs[1]
        new_up = jnp.dot(above_t, upper, precision=lax.Precision.HIGHEST)
        new_low = jnp.dot(below_t, lower, precision=lax.Precision.HIGHEST)
        new_up = unit_scaled(new_up).astype(jnp.bfloat16)
        new_low = unit_scaled(new_low).astype(jnp.bfloat16)
        if step + 1 < STEPS:
            up_corner_nb = shifted(new_up, 1, -1)
            low_corner_nb = shifted(new_low, 1, 1)
        edge_new = edge_contract(west_edge, below_t.astype(jnp.bfloat16), above_t.astype(jnp.bfloat16), site)
        edge_new = unit_scaled(edge_new).astype(jnp.bfloat16)
        corner_up, west_edge, corner_low = shifted((new_up, edge_new, new_low), 1, 0)
    return (corner_up[None, None], west_edge[None, None], corner_low[None, None])


def solution(mesh):
    return jax.shard_map(
        per_device,
        mesh=mesh,
        in_specs=(
            P("gx", "gy", None, None),
            P("gx", "gy", None, None),
            P("gx", "gy", None, None),
            P("gx", "gy", None, None),
            P("gx", "gy", None, None),
            P("gx", "gy", None, None),
            P(),
            P(),
        ),
        out_specs=(P("gx", "gy", None, None), P("gx", "gy", None, None), P("gx", "gy", None, None)),
        check_vma=False,
    )
```

```python
import math

import jax
import jax.numpy as jnp
from jax import lax
from jax.experimental import pallas as pl
from jax.experimental.pallas import tpu as pltpu
from jax.sharding import PartitionSpec as P

NS_ITERS = 6
STEPS = 2
LANES = 128


def passed_along(shard, axis, by):
    peers = lax.axis_size(axis)
    return lax.ppermute(shard, axis, [(i, (i + by) % peers) for i in range(peers)])


def split_bf16(x):
    hi = x.astype(jnp.bfloat16)
    return hi, (x - hi.astype(jnp.float32)).astype(jnp.bfloat16)


def dot3(a, b, dims):
    ah, al = split_bf16(a)
    bh, bl = split_bf16(b)
    out = lambda p, q: lax.dot_general(p, q, (dims, ((), ())), preferred_element_type=jnp.float32)
    return out(ah, bh) + (out(ah, bl) + out(al, bh))


def gram3(y):
    yh, yl = split_bf16(y)
    out = lambda p, q: lax.dot_general(p, q, (((1,), (1,)), ((), ())), preferred_element_type=jnp.float32)
    cross = out(yh, yl)
    return out(yh, yh) + (cross + cross.T)


def polar_kernel(y_ref, o_ref, h_ref):
    count = y_ref.shape[0]
    ys = []
    for b in range(count):
        y = y_ref[b]
        ys.append(y / jnp.sqrt(jnp.sum(y * y) + 1e-06))
    for sweep in range(NS_ITERS):
        grams = [gram3(y) for y in ys]
        ys = [1.5 * y - 0.5 * dot3(g, y, ((1,), (0,))) for g, y in zip(grams, ys)]
    for b in range(count):
        o_ref[b] = ys[b]
        h_ref[b] = ys[b].astype(h_ref.dtype)


def polar_factor_t(stack):
    return pl.pallas_call(
        polar_kernel,
        out_shape=(
            jax.ShapeDtypeStruct(stack.shape, jnp.float32),
            jax.ShapeDtypeStruct(stack.shape, jnp.bfloat16),
        ),
        compiler_params=pltpu.CompilerParams(vmem_limit_bytes=32 * 1024 * 1024),
    )(stack)


def shifted(tree, dx, dy):
    nx = lax.axis_size("gx")
    ny = lax.axis_size("gy")
    pairs = []
    for x in range(nx):
        for y in range(ny):
            pairs.append((x * ny + y, ((x + dx) % nx) * ny + (y + dy) % ny))
    return lax.ppermute(tree, ("gx", "gy"), pairs)


def unit_scaled(tensor):
    return tensor / jnp.sqrt(jnp.mean(tensor * tensor) + 1e-06)


def edge_kernel(wd_ref, pm_ref, t_ref, qt_ref, o_ref, f_ref, g_ref):
    n = qt_ref.shape[0]
    dd = o_ref.shape[0]
    group = 4
    wd = wd_ref[...]
    for d0 in range(0, dd, group):
        part = jnp.dot(wd, pm_ref[:, d0 * LANES:(d0 + group) * LANES], preferred_element_type=jnp.float32)
        part = part.astype(jnp.bfloat16)
        for k in range(group):
            f_ref[:, d0 + k] = part[:, k * LANES:(k + 1) * LANES].reshape(n, dd, LANES)
    t = t_ref[...]
    per = math.gcd(n, 48)

    def mid_body(h, carry):
        x = jnp.concatenate([f_ref[h * per + k].reshape(dd * dd, LANES) for k in range(per)], axis=1)
        g = jnp.dot(t, x, preferred_element_type=jnp.float32).astype(jnp.bfloat16)
        for k in range(per):
            at = pl.multiple_of((h * per + k) * dd, dd)
            for r in range(dd):
                g_ref[pl.ds(at, dd), r * LANES:(r + 1) * LANES] = g[r * dd:(r + 1) * dd, k * LANES:(k + 1) * LANES]
        return carry

    lax.fori_loop(0, n // per, mid_body, 0)
    qt = qt_ref[...]
    for r0 in range(0, dd, group):
        part = jnp.dot(qt, g_ref[:, r0 * LANES:(r0 + group) * LANES], preferred_element_type=jnp.float32)
        for k in range(group):
            o_ref[r0 + k] = part[:, k * LANES:(k + 1) * LANES]


def edge_contract(west, low_t, up_t, site):
    n = west.shape[0]
    dd = west.shape[1] // n
    wd = west.reshape(n * dd, n)
    pm = jnp.transpose(low_t.reshape(n, n, dd), (1, 2, 0))
    pm = jnp.pad(pm, ((0, 0), (0, 0), (0, LANES - n))).reshape(n, dd * LANES)
    qt = up_t
    out = pl.pallas_call(
        edge_kernel,
        out_shape=jax.ShapeDtypeStruct((dd, n, LANES), jnp.float32),
        scratch_shapes=[
            pltpu.VMEM((n, dd, dd, LANES), jnp.bfloat16),
            pltpu.VMEM((n * dd, dd * LANES), jnp.bfloat16),
        ],
        compiler_params=pltpu.CompilerParams(vmem_limit_bytes=48 * 1024 * 1024),
    )(wd, pm, site, qt)
    return jnp.transpose(out[:, :, :n], (1, 0, 2)).reshape(n, dd * n)


def one_hot(rows, cols, row_key, col_key):
    r = lax.broadcasted_iota(jnp.int32, (rows, cols), 0)
    c = lax.broadcasted_iota(jnp.int32, (rows, cols), 1)
    return (row_key(r) == col_key(c)).astype(jnp.float32)


def double_layer(ket, bra):
    q = ket.shape[1]
    dd = q * q
    size = dd * dd
    ket_m = jnp.transpose(ket.astype(jnp.float32), (0, 3, 2, 4, 1)).reshape(ket.shape[0], dd, dd)
    bra_m = jnp.transpose(bra.astype(jnp.float32), (0, 3, 2, 4, 1)).reshape(bra.shape[0], dd, dd)
    k_row = one_hot(size, dd, lambda r: (r // (q * dd)) * q + (r // q) % q, lambda c: c)
    b_row = one_hot(size, dd, lambda r: ((r // dd) % q) * q + r % q, lambda c: c)
    k_col = one_hot(dd, size, lambda r: r, lambda c: (c // (q * dd)) * q + (c // q) % q)
    b_col = one_hot(dd, size, lambda r: r, lambda c: ((c // dd) % q) * q + c % q)
    hi = lax.Precision.HIGHEST
    ket_wide = jnp.einsum("ra,sab,bc->src", k_row, ket_m, k_col, precision=hi)
    bra_wide = jnp.einsum("ra,sab,bc->src", b_row, bra_m, b_col, precision=hi)
    return jnp.sum(ket_wide * bra_wide, axis=0).astype(jnp.bfloat16)


def per_device(
    c_upper, edge_upper, edge_left, c_lower, edge_lower, site_ket, time_gate, quench_sites
):
    env_width = c_upper.shape[-1]
    double_bond = edge_upper.shape[-1] // env_width
    bond_dim = math.isqrt(double_bond)
    phys_dim = site_ket.shape[2]
    ket_sites = site_ket[0, 0].reshape(phys_dim, bond_dim, bond_dim, bond_dim, bond_dim)
    gram = jnp.dot(time_gate.T, time_gate, precision=lax.Precision.HIGHEST)
    gated = jnp.einsum(
        "st,tabcd->sabcd", gram, ket_sites.astype(jnp.float32), precision=lax.Precision.HIGHEST
    )
    own_index = lax.axis_index("gx") * lax.axis_size("gy") + lax.axis_index("gy")
    chosen = jnp.any(quench_sites == own_index)
    bra = jnp.where(chosen, gated, ket_sites.astype(jnp.float32)).astype(jnp.bfloat16)
    site = double_layer(ket_sites, bra)
    north_edge = edge_upper[0, 0]
    south_edge = edge_lower[0, 0]
    corner_up = c_upper[0, 0]
    west_edge = edge_left[0, 0]
    corner_low = c_lower[0, 0]
    up_corner_nb, north_nb = shifted((corner_up, north_edge), 0, -1)
    low_corner_nb, south_nb = shifted((corner_low, south_edge), 0, 1)
    n = env_width
    for step in range(STEPS):
        def half(corner, edge):
            return jnp.dot(corner, edge, preferred_element_type=jnp.float32).reshape(n * double_bond, n)

        upper = half(corner_up, north_edge)
        lower = half(corner_low, south_edge)
        upper_nb = half(up_corner_nb, north_nb)
        lower_nb = half(low_corner_nb, south_nb)
        projs, projs16 = polar_factor_t(jnp.swapaxes(jnp.stack([lower + upper_nb, lower_nb + upper]), 1, 2))
        below_t = projs[0]
        above_t = projs[1]
        new_up = jnp.dot(above_t, upper, precision=lax.Precision.HIGHEST)
        new_low = jnp.dot(below_t, lower, precision=lax.Precision.HIGHEST)
        new_up = unit_scaled(new_up).astype(jnp.bfloat16)
        new_low = unit_scaled(new_low).astype(jnp.bfloat16)
        if step + 1 < STEPS:
            up_corner_nb = shifted(new_up, 1, -1)
            low_corner_nb = shifted(new_low, 1, 1)
        edge_new = edge_contract(west_edge, projs16[0], projs16[1], site)
        edge_new = unit_scaled(edge_new).astype(jnp.bfloat16)
        corner_up, west_edge, corner_low = shifted((new_up, edge_new, new_low), 1, 0)
    return (corner_up[None, None], west_edge[None, None], corner_low[None, None])


def solution(mesh):
    return jax.shard_map(
        per_device,
        mesh=mesh,
        in_specs=(
            P("gx", "gy", None, None),
            P("gx", "gy", None, None),
            P("gx", "gy", None, None),
            P("gx", "gy", None, None),
            P("gx", "gy", None, None),
            P("gx", "gy", None, None),
            P(),
            P(),
        ),
        out_specs=(P("gx", "gy", None, None), P("gx", "gy", None, None), P("gx", "gy", None, None)),
        check_vma=False,
    )
```

```python
import math

import jax
import jax.numpy as jnp
from jax import lax
from jax.experimental import pallas as pl
from jax.experimental.pallas import tpu as pltpu
from jax.sharding import PartitionSpec as P

NS_ITERS = 6
STEPS = 2
LANES = 128


def passed_along(shard, axis, by):
    peers = lax.axis_size(axis)
    return lax.ppermute(shard, axis, [(i, (i + by) % peers) for i in range(peers)])


def split_bf16(x):
    hi = x.astype(jnp.bfloat16)
    return hi, (x - hi.astype(jnp.float32)).astype(jnp.bfloat16)


def dot3(a, b, dims):
    ah, al = split_bf16(a)
    bh, bl = split_bf16(b)
    out = lambda p, q: lax.dot_general(p, q, (dims, ((), ())), preferred_element_type=jnp.float32)
    return out(ah, bh) + (out(ah, bl) + out(al, bh))


def gram3(y):
    yh, yl = split_bf16(y)
    out = lambda p, q: lax.dot_general(p, q, (((1,), (1,)), ((), ())), preferred_element_type=jnp.float32)
    cross = out(yh, yl)
    return out(yh, yh) + (cross + cross.T)


def polar_kernel(y_ref, o_ref, h_ref):
    count = y_ref.shape[0]
    ys = []
    for b in range(count):
        y = y_ref[b]
        ys.append(y / jnp.sqrt(jnp.sum(y * y) + 1e-06))
    for sweep in range(NS_ITERS):
        grams = [gram3(y) for y in ys]
        ys = [1.5 * y - 0.5 * dot3(g, y, ((1,), (0,))) for g, y in zip(grams, ys)]
    for b in range(count):
        o_ref[b] = ys[b]
        h_ref[b] = ys[b].astype(h_ref.dtype)


def polar_factor_t(stack):
    return pl.pallas_call(
        polar_kernel,
        out_shape=(
            jax.ShapeDtypeStruct(stack.shape, jnp.float32),
            jax.ShapeDtypeStruct(stack.shape, jnp.bfloat16),
        ),
        compiler_params=pltpu.CompilerParams(vmem_limit_bytes=32 * 1024 * 1024),
    )(stack)


def shifted(tree, dx, dy):
    nx = lax.axis_size("gx")
    ny = lax.axis_size("gy")
    pairs = []
    for x in range(nx):
        for y in range(ny):
            pairs.append((x * ny + y, ((x + dx) % nx) * ny + (y + dy) % ny))
    return lax.ppermute(tree, ("gx", "gy"), pairs)


def unit_scaled(tensor):
    return tensor / jnp.sqrt(jnp.mean(tensor * tensor) + 1e-06)


def edge_kernel(wd_ref, pm_ref, t_ref, qt_ref, o_ref, f_ref, g_ref):
    n = qt_ref.shape[0]
    dd = o_ref.shape[0]
    group = 4
    wd = wd_ref[...]
    for d0 in range(0, dd, group):
        part = jnp.dot(wd, pm_ref[:, d0 * LANES:(d0 + group) * LANES], preferred_element_type=jnp.float32)
        part = part.astype(jnp.bfloat16)
        for k in range(group):
            f_ref[:, d0 + k] = part[:, k * LANES:(k + 1) * LANES].reshape(n, dd, LANES)
    t = t_ref[...]
    per = math.gcd(n, 48)

    def mid_body(h, carry):
        x = jnp.concatenate([f_ref[h * per + k].reshape(dd * dd, LANES) for k in range(per)], axis=1)
        g = jnp.dot(t, x, preferred_element_type=jnp.float32).astype(jnp.bfloat16)
        for k in range(per):
            at = pl.multiple_of((h * per + k) * dd, dd)
            for r in range(dd):
                g_ref[pl.ds(at, dd), r * LANES:(r + 1) * LANES] = g[r * dd:(r + 1) * dd, k * LANES:(k + 1) * LANES]
        return carry

    lax.fori_loop(0, n // per, mid_body, 0)
    qt = qt_ref[...]
    for r0 in range(0, dd, group):
        part = jnp.dot(qt, g_ref[:, r0 * LANES:(r0 + group) * LANES], preferred_element_type=jnp.float32)
        for k in range(group):
            o_ref[r0 + k] = part[:, k * LANES:(k + 1) * LANES]


def edge_contract(west, low_t, up_t, site):
    n = west.shape[0]
    dd = west.shape[1] // n
    wd = west.reshape(n * dd, n)
    pm = jnp.transpose(low_t.reshape(n, n, dd), (1, 2, 0))
    pm = jnp.pad(pm, ((0, 0), (0, 0), (0, LANES - n))).reshape(n, dd * LANES)
    qt = up_t
    out = pl.pallas_call(
        edge_kernel,
        out_shape=jax.ShapeDtypeStruct((dd, n, LANES), jnp.float32),
        scratch_shapes=[
            pltpu.VMEM((n, dd, dd, LANES), jnp.bfloat16),
            pltpu.VMEM((n * dd, dd * LANES), jnp.bfloat16),
        ],
        compiler_params=pltpu.CompilerParams(vmem_limit_bytes=48 * 1024 * 1024),
    )(wd, pm, site, qt)
    return jnp.transpose(out[:, :, :n], (1, 0, 2)).reshape(n, dd * n)


def one_hot(rows, cols, row_key, col_key):
    r = lax.broadcasted_iota(jnp.int32, (rows, cols), 0)
    c = lax.broadcasted_iota(jnp.int32, (rows, cols), 1)
    return (row_key(r) == col_key(c)).astype(jnp.float32)


def double_layer(ket, bra):
    q = ket.shape[1]
    dd = q * q
    size = dd * dd
    ket_m = jnp.transpose(ket.astype(jnp.float32), (0, 3, 2, 4, 1)).reshape(ket.shape[0], dd, dd)
    bra_m = jnp.transpose(bra.astype(jnp.float32), (0, 3, 2, 4, 1)).reshape(bra.shape[0], dd, dd)
    k_row = one_hot(size, dd, lambda r: (r // (q * dd)) * q + (r // q) % q, lambda c: c)
    b_row = one_hot(size, dd, lambda r: ((r // dd) % q) * q + r % q, lambda c: c)
    k_col = one_hot(dd, size, lambda r: r, lambda c: (c // (q * dd)) * q + (c // q) % q)
    b_col = one_hot(dd, size, lambda r: r, lambda c: ((c // dd) % q) * q + c % q)
    hi = lax.Precision.HIGHEST
    ket_wide = jnp.einsum("ra,sab,bc->src", k_row, ket_m, k_col, precision=hi)
    bra_wide = jnp.einsum("ra,sab,bc->src", b_row, bra_m, b_col, precision=hi)
    return jnp.sum(ket_wide * bra_wide, axis=0).astype(jnp.bfloat16)


def per_device(
    c_upper, edge_upper, edge_left, c_lower, edge_lower, site_ket, time_gate, quench_sites
):
    env_width = c_upper.shape[-1]
    double_bond = edge_upper.shape[-1] // env_width
    bond_dim = math.isqrt(double_bond)
    phys_dim = site_ket.shape[2]
    ket_sites = site_ket[0, 0].reshape(phys_dim, bond_dim, bond_dim, bond_dim, bond_dim)
    gram = jnp.dot(time_gate.T, time_gate, precision=lax.Precision.HIGHEST)
    gated = jnp.einsum(
        "st,tabcd->sabcd", gram, ket_sites.astype(jnp.float32), precision=lax.Precision.HIGHEST
    )
    own_index = lax.axis_index("gx") * lax.axis_size("gy") + lax.axis_index("gy")
    chosen = jnp.any(quench_sites == own_index)
    bra = jnp.where(chosen, gated, ket_sites.astype(jnp.float32)).astype(jnp.bfloat16)
    site = double_layer(ket_sites, bra)
    north_edge = edge_upper[0, 0]
    south_edge = edge_lower[0, 0]
    corner_up = c_upper[0, 0]
    west_edge = edge_left[0, 0]
    corner_low = c_lower[0, 0]
    up_corner_nb, north_nb = shifted((corner_up, north_edge), 0, -1)
    low_corner_nb, south_nb = shifted((corner_low, south_edge), 0, 1)
    n = env_width
    for step in range(STEPS):
        def half(corner, edge):
            return jnp.dot(corner, edge, preferred_element_type=jnp.float32).reshape(n * double_bond, n)

        upper = half(corner_up, north_edge)
        lower = half(corner_low, south_edge)
        upper_nb = half(up_corner_nb, north_nb)
        lower_nb = half(low_corner_nb, south_nb)
        projs, projs16 = polar_factor_t(jnp.swapaxes(jnp.stack([lower + upper_nb, lower_nb + upper]), 1, 2))
        below_t = projs[0]
        above_t = projs[1]
        new_up = jnp.dot(above_t, upper, precision=lax.Precision.HIGH)
        new_low = jnp.dot(below_t, lower, precision=lax.Precision.HIGH)
        new_up = unit_scaled(new_up).astype(jnp.bfloat16)
        new_low = unit_scaled(new_low).astype(jnp.bfloat16)
        if step + 1 < STEPS:
            up_corner_nb = shifted(new_up, 1, -1)
            low_corner_nb = shifted(new_low, 1, 1)
        edge_new = edge_contract(west_edge, projs16[0], projs16[1], site)
        edge_new = unit_scaled(edge_new).astype(jnp.bfloat16)
        corner_up, west_edge, corner_low = shifted((new_up, edge_new, new_low), 1, 0)
    return (corner_up[None, None], west_edge[None, None], corner_low[None, None])


def solution(mesh):
    return jax.shard_map(
        per_device,
        mesh=mesh,
        in_specs=(
            P("gx", "gy", None, None),
            P("gx", "gy", None, None),
            P("gx", "gy", None, None),
            P("gx", "gy", None, None),
            P("gx", "gy", None, None),
            P("gx", "gy", None, None),
            P(),
            P(),
        ),
        out_specs=(P("gx", "gy", None, None), P("gx", "gy", None, None), P("gx", "gy", None, None)),
        check_vma=False,
    )
```

```python
import math

import jax
import jax.numpy as jnp
from jax import lax
from jax.experimental import pallas as pl
from jax.experimental.pallas import tpu as pltpu
from jax.sharding import PartitionSpec as P

NS_ITERS = 6
STEPS = 2
LANES = 128


def passed_along(shard, axis, by):
    peers = lax.axis_size(axis)
    return lax.ppermute(shard, axis, [(i, (i + by) % peers) for i in range(peers)])


def split_bf16(x):
    hi = x.astype(jnp.bfloat16)
    return hi, (x - hi.astype(jnp.float32)).astype(jnp.bfloat16)


def dot3(a, b, dims):
    ah, al = split_bf16(a)
    bh, bl = split_bf16(b)
    out = lambda p, q: lax.dot_general(p, q, (dims, ((), ())), preferred_element_type=jnp.float32)
    return out(ah, bh) + (out(ah, bl) + out(al, bh))


def gram3(y):
    yh, yl = split_bf16(y)
    out = lambda p, q: lax.dot_general(p, q, (((1,), (1,)), ((), ())), preferred_element_type=jnp.float32)
    cross = out(yh, yl)
    return out(yh, yh) + (cross + cross.T)


def polar_kernel(y_ref, o_ref, h_ref):
    count = y_ref.shape[0]
    ys = []
    for b in range(count):
        y = y_ref[b]
        ys.append(y / jnp.sqrt(jnp.sum(y * y) + 1e-06))
    for sweep in range(NS_ITERS):
        grams = [gram3(y) for y in ys]
        ys = [1.5 * y - 0.5 * dot3(g, y, ((1,), (0,))) for g, y in zip(grams, ys)]
    for b in range(count):
        o_ref[b] = ys[b]
        h_ref[b] = ys[b].astype(h_ref.dtype)


def polar_factor_t(stack):
    return pl.pallas_call(
        polar_kernel,
        out_shape=(
            jax.ShapeDtypeStruct(stack.shape, jnp.float32),
            jax.ShapeDtypeStruct(stack.shape, jnp.bfloat16),
        ),
        compiler_params=pltpu.CompilerParams(vmem_limit_bytes=32 * 1024 * 1024),
    )(stack)


def shifted(tree, dx, dy):
    nx = lax.axis_size("gx")
    ny = lax.axis_size("gy")
    pairs = []
    for x in range(nx):
        for y in range(ny):
            pairs.append((x * ny + y, ((x + dx) % nx) * ny + (y + dy) % ny))
    return lax.ppermute(tree, ("gx", "gy"), pairs)


def unit_scaled(tensor):
    return tensor / jnp.sqrt(jnp.mean(tensor * tensor) + 1e-06)


def edge_kernel(wd_ref, pm_ref, t_ref, qt_ref, o_ref, f_ref, g_ref):
    n = qt_ref.shape[0]
    dd = o_ref.shape[0]
    group = 4
    wd = wd_ref[...]
    for d0 in range(0, dd, group):
        part = jnp.dot(wd, pm_ref[:, d0 * LANES:(d0 + group) * LANES], preferred_element_type=jnp.float32)
        part = part.astype(jnp.bfloat16)
        for k in range(group):
            f_ref[:, d0 + k] = part[:, k * LANES:(k + 1) * LANES].reshape(n, dd, LANES)
    t = t_ref[...]
    per = n

    def mid_body(h, carry):
        x = jnp.concatenate([f_ref[h * per + k].reshape(dd * dd, LANES) for k in range(per)], axis=1)
        g = jnp.dot(t, x, preferred_element_type=jnp.float32).astype(jnp.bfloat16)
        for k in range(per):
            at = pl.multiple_of((h * per + k) * dd, dd)
            for r in range(dd):
                g_ref[pl.ds(at, dd), r * LANES:(r + 1) * LANES] = g[r * dd:(r + 1) * dd, k * LANES:(k + 1) * LANES]
        return carry

    lax.fori_loop(0, n // per, mid_body, 0)
    qt = qt_ref[...]
    for r0 in range(0, dd, group):
        part = jnp.dot(qt, g_ref[:, r0 * LANES:(r0 + group) * LANES], preferred_element_type=jnp.float32)
        for k in range(group):
            o_ref[r0 + k] = part[:, k * LANES:(k + 1) * LANES]


def edge_contract(west, low_t, up_t, site):
    n = west.shape[0]
    dd = west.shape[1] // n
    wd = west.reshape(n * dd, n)
    pm = jnp.transpose(low_t.reshape(n, n, dd), (1, 2, 0))
    pm = jnp.pad(pm, ((0, 0), (0, 0), (0, LANES - n))).reshape(n, dd * LANES)
    qt = up_t
    out = pl.pallas_call(
        edge_kernel,
        out_shape=jax.ShapeDtypeStruct((dd, n, LANES), jnp.float32),
        scratch_shapes=[
            pltpu.VMEM((n, dd, dd, LANES), jnp.bfloat16),
            pltpu.VMEM((n * dd, dd * LANES), jnp.bfloat16),
        ],
        compiler_params=pltpu.CompilerParams(vmem_limit_bytes=48 * 1024 * 1024),
    )(wd, pm, site, qt)
    return jnp.transpose(out[:, :, :n], (1, 0, 2)).reshape(n, dd * n)


def one_hot(rows, cols, row_key, col_key):
    r = lax.broadcasted_iota(jnp.int32, (rows, cols), 0)
    c = lax.broadcasted_iota(jnp.int32, (rows, cols), 1)
    return (row_key(r) == col_key(c)).astype(jnp.float32)


def double_layer(ket, bra):
    q = ket.shape[1]
    dd = q * q
    size = dd * dd
    ket_m = jnp.transpose(ket.astype(jnp.float32), (0, 3, 2, 4, 1)).reshape(ket.shape[0], dd, dd)
    bra_m = jnp.transpose(bra.astype(jnp.float32), (0, 3, 2, 4, 1)).reshape(bra.shape[0], dd, dd)
    k_row = one_hot(size, dd, lambda r: (r // (q * dd)) * q + (r // q) % q, lambda c: c)
    b_row = one_hot(size, dd, lambda r: ((r // dd) % q) * q + r % q, lambda c: c)
    k_col = one_hot(dd, size, lambda r: r, lambda c: (c // (q * dd)) * q + (c // q) % q)
    b_col = one_hot(dd, size, lambda r: r, lambda c: ((c // dd) % q) * q + c % q)
    hi = lax.Precision.HIGHEST
    ket_wide = jnp.einsum("ra,sab,bc->src", k_row, ket_m, k_col, precision=hi)
    bra_wide = jnp.einsum("ra,sab,bc->src", b_row, bra_m, b_col, precision=hi)
    return jnp.sum(ket_wide * bra_wide, axis=0).astype(jnp.bfloat16)


def per_device(
    c_upper, edge_upper, edge_left, c_lower, edge_lower, site_ket, time_gate, quench_sites
):
    env_width = c_upper.shape[-1]
    double_bond = edge_upper.shape[-1] // env_width
    bond_dim = math.isqrt(double_bond)
    phys_dim = site_ket.shape[2]
    ket_sites = site_ket[0, 0].reshape(phys_dim, bond_dim, bond_dim, bond_dim, bond_dim)
    gram = jnp.dot(time_gate.T, time_gate, precision=lax.Precision.HIGHEST)
    gated = jnp.einsum(
        "st,tabcd->sabcd", gram, ket_sites.astype(jnp.float32), precision=lax.Precision.HIGHEST
    )
    own_index = lax.axis_index("gx") * lax.axis_size("gy") + lax.axis_index("gy")
    chosen = jnp.any(quench_sites == own_index)
    bra = jnp.where(chosen, gated, ket_sites.astype(jnp.float32)).astype(jnp.bfloat16)
    site = double_layer(ket_sites, bra)
    north_edge = edge_upper[0, 0]
    south_edge = edge_lower[0, 0]
    corner_up = c_upper[0, 0]
    west_edge = edge_left[0, 0]
    corner_low = c_lower[0, 0]
    up_corner_nb, north_nb = shifted((corner_up, north_edge), 0, -1)
    low_corner_nb, south_nb = shifted((corner_low, south_edge), 0, 1)
    n = env_width
    for step in range(STEPS):
        def half(corner, edge):
            return jnp.dot(corner, edge, preferred_element_type=jnp.float32).reshape(n * double_bond, n)

        upper = half(corner_up, north_edge)
        lower = half(corner_low, south_edge)
        upper_nb = half(up_corner_nb, north_nb)
        lower_nb = half(low_corner_nb, south_nb)
        projs, projs16 = polar_factor_t(jnp.swapaxes(jnp.stack([lower + upper_nb, lower_nb + upper]), 1, 2))
        below_t = projs[0]
        above_t = projs[1]
        new_up = jnp.dot(above_t, upper, precision=lax.Precision.HIGH)
        new_low = jnp.dot(below_t, lower, precision=lax.Precision.HIGH)
        new_up = unit_scaled(new_up).astype(jnp.bfloat16)
        new_low = unit_scaled(new_low).astype(jnp.bfloat16)
        if step + 1 < STEPS:
            up_corner_nb = shifted(new_up, 1, -1)
            low_corner_nb = shifted(new_low, 1, 1)
        edge_new = edge_contract(west_edge, projs16[0], projs16[1], site)
        edge_new = unit_scaled(edge_new).astype(jnp.bfloat16)
        corner_up, west_edge, corner_low = shifted((new_up, edge_new, new_low), 1, 0)
    return (corner_up[None, None], west_edge[None, None], corner_low[None, None])


def solution(mesh):
    return jax.shard_map(
        per_device,
        mesh=mesh,
        in_specs=(
            P("gx", "gy", None, None),
            P("gx", "gy", None, None),
            P("gx", "gy", None, None),
            P("gx", "gy", None, None),
            P("gx", "gy", None, None),
            P("gx", "gy", None, None),
            P(),
            P(),
        ),
        out_specs=(P("gx", "gy", None, None), P("gx", "gy", None, None), P("gx", "gy", None, None)),
        check_vma=False,
    )
```

```python
import math

import jax
import jax.numpy as jnp
from jax import lax
from jax.experimental import pallas as pl
from jax.experimental.pallas import tpu as pltpu
from jax.sharding import PartitionSpec as P

NS_ITERS = 6
STEPS = 2
LANES = 128


def passed_along(shard, axis, by):
    peers = lax.axis_size(axis)
    return lax.ppermute(shard, axis, [(i, (i + by) % peers) for i in range(peers)])


def split_bf16(x):
    hi = x.astype(jnp.bfloat16)
    return hi, (x - hi.astype(jnp.float32)).astype(jnp.bfloat16)


def dot3(a, b, dims):
    ah, al = split_bf16(a)
    bh, bl = split_bf16(b)
    out = lambda p, q: lax.dot_general(p, q, (dims, ((), ())), preferred_element_type=jnp.float32)
    return out(ah, bh) + (out(ah, bl) + out(al, bh))


def gram3(y):
    yh, yl = split_bf16(y)
    out = lambda p, q: lax.dot_general(p, q, (((1,), (1,)), ((), ())), preferred_element_type=jnp.float32)
    cross = out(yh, yl)
    return out(yh, yh) + (cross + cross.T)


def ns_step(y):
    out = lambda p, q, dims: lax.dot_general(p, q, (dims, ((), ())), preferred_element_type=jnp.float32)
    yh, yl = split_bf16(y)
    cross = out(yh, yl, ((1,), (1,)))
    gram = out(yh, yh, ((1,), (1,))) + (cross + cross.T)
    gh, gl = split_bf16(gram)
    dims = ((1,), (0,))
    return 1.5 * y - 0.5 * (out(gh, yh, dims) + (out(gh, yl, dims) + out(gl, yh, dims)))


def polar_kernel(y_ref, o_ref, h_ref):
    count = y_ref.shape[0]
    ys = []
    for b in range(count):
        y = y_ref[b]
        ys.append(y / jnp.sqrt(jnp.sum(y * y) + 1e-06))
    for sweep in range(NS_ITERS):
        ys = [ns_step(y) for y in ys]
    for b in range(count):
        o_ref[b] = ys[b]
        h_ref[b] = ys[b].astype(h_ref.dtype)


def polar_factor_t(stack):
    return pl.pallas_call(
        polar_kernel,
        out_shape=(
            jax.ShapeDtypeStruct(stack.shape, jnp.float32),
            jax.ShapeDtypeStruct(stack.shape, jnp.bfloat16),
        ),
        compiler_params=pltpu.CompilerParams(vmem_limit_bytes=32 * 1024 * 1024),
    )(stack)


def shifted(tree, dx, dy):
    nx = lax.axis_size("gx")
    ny = lax.axis_size("gy")
    pairs = []
    for x in range(nx):
        for y in range(ny):
            pairs.append((x * ny + y, ((x + dx) % nx) * ny + (y + dy) % ny))
    return lax.ppermute(tree, ("gx", "gy"), pairs)


def unit_scaled(tensor):
    return tensor / jnp.sqrt(jnp.mean(tensor * tensor) + 1e-06)


def edge_kernel(wd_ref, pm_ref, t_ref, qt_ref, o_ref, f_ref, g_ref):
    n = qt_ref.shape[0]
    dd = o_ref.shape[0]
    group = 4
    wd = wd_ref[...]
    for d0 in range(0, dd, group):
        part = jnp.dot(wd, pm_ref[:, d0 * LANES:(d0 + group) * LANES], preferred_element_type=jnp.float32)
        part = part.astype(jnp.bfloat16)
        for k in range(group):
            f_ref[:, d0 + k] = part[:, k * LANES:(k + 1) * LANES].reshape(n, dd, LANES)
    t = t_ref[...]
    per = n

    def mid_body(h, carry):
        x = jnp.concatenate([f_ref[h * per + k].reshape(dd * dd, LANES) for k in range(per)], axis=1)
        g = jnp.dot(t, x, preferred_element_type=jnp.float32).astype(jnp.bfloat16)
        for k in range(per):
            at = pl.multiple_of((h * per + k) * dd, dd)
            for r in range(dd):
                g_ref[pl.ds(at, dd), r * LANES:(r + 1) * LANES] = g[r * dd:(r + 1) * dd, k * LANES:(k + 1) * LANES]
        return carry

    lax.fori_loop(0, n // per, mid_body, 0)
    qt = qt_ref[...]
    for r0 in range(0, dd, group):
        part = jnp.dot(qt, g_ref[:, r0 * LANES:(r0 + group) * LANES], preferred_element_type=jnp.float32)
        for k in range(group):
            o_ref[r0 + k] = part[:, k * LANES:(k + 1) * LANES]


def edge_contract(west, low_t, up_t, site):
    n = west.shape[0]
    dd = west.shape[1] // n
    wd = west.reshape(n * dd, n)
    pm = jnp.transpose(low_t.reshape(n, n, dd), (1, 2, 0))
    pm = jnp.pad(pm, ((0, 0), (0, 0), (0, LANES - n))).reshape(n, dd * LANES)
    qt = up_t
    out = pl.pallas_call(
        edge_kernel,
        out_shape=jax.ShapeDtypeStruct((dd, n, LANES), jnp.float32),
        scratch_shapes=[
            pltpu.VMEM((n, dd, dd, LANES), jnp.bfloat16),
            pltpu.VMEM((n * dd, dd * LANES), jnp.bfloat16),
        ],
        compiler_params=pltpu.CompilerParams(vmem_limit_bytes=48 * 1024 * 1024),
    )(wd, pm, site, qt)
    return jnp.transpose(out[:, :, :n], (1, 0, 2)).reshape(n, dd * n)


def one_hot(rows, cols, row_key, col_key):
    r = lax.broadcasted_iota(jnp.int32, (rows, cols), 0)
    c = lax.broadcasted_iota(jnp.int32, (rows, cols), 1)
    return (row_key(r) == col_key(c)).astype(jnp.float32)


def double_layer(ket, bra):
    q = ket.shape[1]
    dd = q * q
    size = dd * dd
    ket_m = jnp.transpose(ket.astype(jnp.float32), (0, 3, 2, 4, 1)).reshape(ket.shape[0], dd, dd)
    bra_m = jnp.transpose(bra.astype(jnp.float32), (0, 3, 2, 4, 1)).reshape(bra.shape[0], dd, dd)
    k_row = one_hot(size, dd, lambda r: (r // (q * dd)) * q + (r // q) % q, lambda c: c)
    b_row = one_hot(size, dd, lambda r: ((r // dd) % q) * q + r % q, lambda c: c)
    k_col = one_hot(dd, size, lambda r: r, lambda c: (c // (q * dd)) * q + (c // q) % q)
    b_col = one_hot(dd, size, lambda r: r, lambda c: ((c // dd) % q) * q + c % q)
    hi = lax.Precision.HIGHEST
    ket_wide = jnp.einsum("ra,sab,bc->src", k_row, ket_m, k_col, precision=hi)
    bra_wide = jnp.einsum("ra,sab,bc->src", b_row, bra_m, b_col, precision=hi)
    return jnp.sum(ket_wide * bra_wide, axis=0).astype(jnp.bfloat16)


def per_device(
    c_upper, edge_upper, edge_left, c_lower, edge_lower, site_ket, time_gate, quench_sites
):
    env_width = c_upper.shape[-1]
    double_bond = edge_upper.shape[-1] // env_width
    bond_dim = math.isqrt(double_bond)
    phys_dim = site_ket.shape[2]
    ket_sites = site_ket[0, 0].reshape(phys_dim, bond_dim, bond_dim, bond_dim, bond_dim)
    gram = jnp.dot(time_gate.T, time_gate, precision=lax.Precision.HIGHEST)
    gated = jnp.einsum(
        "st,tabcd->sabcd", gram, ket_sites.astype(jnp.float32), precision=lax.Precision.HIGHEST
    )
    own_index = lax.axis_index("gx") * lax.axis_size("gy") + lax.axis_index("gy")
    chosen = jnp.any(quench_sites == own_index)
    bra = jnp.where(chosen, gated, ket_sites.astype(jnp.float32)).astype(jnp.bfloat16)
    site = double_layer(ket_sites, bra)
    north_edge = edge_upper[0, 0]
    south_edge = edge_lower[0, 0]
    corner_up = c_upper[0, 0]
    west_edge = edge_left[0, 0]
    corner_low = c_lower[0, 0]
    up_corner_nb, north_nb = shifted((corner_up, north_edge), 0, -1)
    low_corner_nb, south_nb = shifted((corner_low, south_edge), 0, 1)
    n = env_width
    for step in range(STEPS):
        def half(corner, edge):
            return jnp.dot(corner, edge, preferred_element_type=jnp.float32).reshape(n * double_bond, n)

        upper = half(corner_up, north_edge)
        lower = half(corner_low, south_edge)
        upper_nb = half(up_corner_nb, north_nb)
        lower_nb = half(low_corner_nb, south_nb)
        projs, projs16 = polar_factor_t(jnp.swapaxes(jnp.stack([lower + upper_nb, lower_nb + upper]), 1, 2))
        below_t = projs[0]
        above_t = projs[1]
        new_up = jnp.dot(above_t, upper, precision=lax.Precision.HIGH)
        new_low = jnp.dot(below_t, lower, precision=lax.Precision.HIGH)
        new_up = unit_scaled(new_up).astype(jnp.bfloat16)
        new_low = unit_scaled(new_low).astype(jnp.bfloat16)
        if step + 1 < STEPS:
            up_corner_nb = shifted(new_up, 1, -1)
            low_corner_nb = shifted(new_low, 1, 1)
        edge_new = edge_contract(west_edge, projs16[0], projs16[1], site)
        edge_new = unit_scaled(edge_new).astype(jnp.bfloat16)
        corner_up, west_edge, corner_low = shifted((new_up, edge_new, new_low), 1, 0)
    return (corner_up[None, None], west_edge[None, None], corner_low[None, None])


def solution(mesh):
    return jax.shard_map(
        per_device,
        mesh=mesh,
        in_specs=(
            P("gx", "gy", None, None),
            P("gx", "gy", None, None),
            P("gx", "gy", None, None),
            P("gx", "gy", None, None),
            P("gx", "gy", None, None),
            P("gx", "gy", None, None),
            P(),
            P(),
        ),
        out_specs=(P("gx", "gy", None, None), P("gx", "gy", None, None), P("gx", "gy", None, None)),
        check_vma=False,
    )
```

```python
import math

import jax
import jax.numpy as jnp
from jax import lax
from jax.experimental import pallas as pl
from jax.experimental.pallas import tpu as pltpu
from jax.sharding import PartitionSpec as P

NS_ITERS = 6
STEPS = 2
LANES = 128


def passed_along(shard, axis, by):
    peers = lax.axis_size(axis)
    return lax.ppermute(shard, axis, [(i, (i + by) % peers) for i in range(peers)])


def split_bf16(x):
    hi = x.astype(jnp.bfloat16)
    return hi, (x - hi.astype(jnp.float32)).astype(jnp.bfloat16)


def dot3(a, b, dims):
    ah, al = split_bf16(a)
    bh, bl = split_bf16(b)
    out = lambda p, q: lax.dot_general(p, q, (dims, ((), ())), preferred_element_type=jnp.float32)
    return out(ah, bh) + (out(ah, bl) + out(al, bh))


def gram3(y):
    yh, yl = split_bf16(y)
    out = lambda p, q: lax.dot_general(p, q, (((1,), (1,)), ((), ())), preferred_element_type=jnp.float32)
    cross = out(yh, yl)
    return out(yh, yh) + (cross + cross.T)


def polar_kernel(y_ref, o_ref, h_ref):
    count = y_ref.shape[0]
    ys = []
    for b in range(count):
        y = y_ref[b]
        ys.append(y / jnp.sqrt(jnp.sum(y * y) + 1e-06))
    for sweep in range(NS_ITERS):
        grams = [gram3(y) for y in ys]
        ys = [1.5 * y - 0.5 * dot3(g, y, ((1,), (0,))) for g, y in zip(grams, ys)]
    for b in range(count):
        o_ref[b] = ys[b]
        h_ref[b] = ys[b].astype(h_ref.dtype)


def polar_factor_t(stack):
    return pl.pallas_call(
        polar_kernel,
        out_shape=(
            jax.ShapeDtypeStruct(stack.shape, jnp.float32),
            jax.ShapeDtypeStruct(stack.shape, jnp.bfloat16),
        ),
        compiler_params=pltpu.CompilerParams(vmem_limit_bytes=32 * 1024 * 1024),
    )(stack)


def shifted(tree, dx, dy):
    nx = lax.axis_size("gx")
    ny = lax.axis_size("gy")
    pairs = []
    for x in range(nx):
        for y in range(ny):
            pairs.append((x * ny + y, ((x + dx) % nx) * ny + (y + dy) % ny))
    return lax.ppermute(tree, ("gx", "gy"), pairs)


def unit_scaled(tensor):
    return tensor / jnp.sqrt(jnp.mean(tensor * tensor) + 1e-06)


def edge_kernel(wd_ref, pm_ref, t_ref, qt_ref, o_ref, f_ref, g_ref):
    n = qt_ref.shape[0]
    dd = o_ref.shape[0]
    group = 4
    wd = wd_ref[...]
    for d0 in range(0, dd, group):
        part = jnp.dot(wd, pm_ref[:, d0 * LANES:(d0 + group) * LANES], preferred_element_type=jnp.float32)
        part = part.astype(jnp.bfloat16)
        for k in range(group):
            f_ref[:, d0 + k] = part[:, k * LANES:(k + 1) * LANES].reshape(n, dd, LANES)
    t = t_ref[...]
    per = n

    def mid_body(h, carry):
        x = jnp.concatenate([f_ref[h * per + k].reshape(dd * dd, LANES) for k in range(per)], axis=1)
        g = jnp.dot(t, x, preferred_element_type=jnp.float32).astype(jnp.bfloat16)
        for k in range(per):
            at = pl.multiple_of((h * per + k) * dd, dd)
            for r in range(dd):
                g_ref[pl.ds(at, dd), r * LANES:(r + 1) * LANES] = g[r * dd:(r + 1) * dd, k * LANES:(k + 1) * LANES]
        return carry

    lax.fori_loop(0, n // per, mid_body, 0)
    qt = qt_ref[...]
    for r0 in range(0, dd, group):
        part = jnp.dot(qt, g_ref[:, r0 * LANES:(r0 + group) * LANES], preferred_element_type=jnp.float32)
        for k in range(group):
            o_ref[r0 + k] = part[:, k * LANES:(k + 1) * LANES]


def edge_contract(west, low_t, up_t, site):
    n = west.shape[0]
    dd = west.shape[1] // n
    wd = west.reshape(n * dd, n)
    pm = jnp.transpose(low_t.reshape(n, n, dd), (1, 2, 0))
    pm = jnp.pad(pm, ((0, 0), (0, 0), (0, LANES - n))).reshape(n, dd * LANES)
    qt = up_t
    out = pl.pallas_call(
        edge_kernel,
        out_shape=jax.ShapeDtypeStruct((dd, n, LANES), jnp.float32),
        scratch_shapes=[
            pltpu.VMEM((n, dd, dd, LANES), jnp.bfloat16),
            pltpu.VMEM((n * dd, dd * LANES), jnp.bfloat16),
        ],
        compiler_params=pltpu.CompilerParams(
            vmem_limit_bytes=48 * 1024 * 1024, allow_input_fusion=[True, True, False, False]
        ),
    )(wd, pm, site, qt)
    return jnp.transpose(out[:, :, :n], (1, 0, 2)).reshape(n, dd * n)


def one_hot(rows, cols, row_key, col_key):
    r = lax.broadcasted_iota(jnp.int32, (rows, cols), 0)
    c = lax.broadcasted_iota(jnp.int32, (rows, cols), 1)
    return (row_key(r) == col_key(c)).astype(jnp.float32)


def double_layer(ket, bra):
    q = ket.shape[1]
    dd = q * q
    size = dd * dd
    ket_m = jnp.transpose(ket.astype(jnp.float32), (0, 3, 2, 4, 1)).reshape(ket.shape[0], dd, dd)
    bra_m = jnp.transpose(bra.astype(jnp.float32), (0, 3, 2, 4, 1)).reshape(bra.shape[0], dd, dd)
    k_row = one_hot(size, dd, lambda r: (r // (q * dd)) * q + (r // q) % q, lambda c: c)
    b_row = one_hot(size, dd, lambda r: ((r // dd) % q) * q + r % q, lambda c: c)
    k_col = one_hot(dd, size, lambda r: r, lambda c: (c // (q * dd)) * q + (c // q) % q)
    b_col = one_hot(dd, size, lambda r: r, lambda c: ((c // dd) % q) * q + c % q)
    hi = lax.Precision.HIGHEST
    ket_wide = jnp.einsum("ra,sab,bc->src", k_row, ket_m, k_col, precision=hi)
    bra_wide = jnp.einsum("ra,sab,bc->src", b_row, bra_m, b_col, precision=hi)
    return jnp.sum(ket_wide * bra_wide, axis=0).astype(jnp.bfloat16)


def per_device(
    c_upper, edge_upper, edge_left, c_lower, edge_lower, site_ket, time_gate, quench_sites
):
    env_width = c_upper.shape[-1]
    double_bond = edge_upper.shape[-1] // env_width
    bond_dim = math.isqrt(double_bond)
    phys_dim = site_ket.shape[2]
    ket_sites = site_ket[0, 0].reshape(phys_dim, bond_dim, bond_dim, bond_dim, bond_dim)
    gram = jnp.dot(time_gate.T, time_gate, precision=lax.Precision.HIGHEST)
    gated = jnp.einsum(
        "st,tabcd->sabcd", gram, ket_sites.astype(jnp.float32), precision=lax.Precision.HIGHEST
    )
    own_index = lax.axis_index("gx") * lax.axis_size("gy") + lax.axis_index("gy")
    chosen = jnp.any(quench_sites == own_index)
    bra = jnp.where(chosen, gated, ket_sites.astype(jnp.float32)).astype(jnp.bfloat16)
    site = double_layer(ket_sites, bra)
    north_edge = edge_upper[0, 0]
    south_edge = edge_lower[0, 0]
    corner_up = c_upper[0, 0]
    west_edge = edge_left[0, 0]
    corner_low = c_lower[0, 0]
    up_corner_nb, north_nb = shifted((corner_up, north_edge), 0, -1)
    low_corner_nb, south_nb = shifted((corner_low, south_edge), 0, 1)
    n = env_width
    for step in range(STEPS):
        def half(corner, edge):
            return jnp.dot(corner, edge, preferred_element_type=jnp.float32).reshape(n * double_bond, n)

        upper = half(corner_up, north_edge)
        lower = half(corner_low, south_edge)
        upper_nb = half(up_corner_nb, north_nb)
        lower_nb = half(low_corner_nb, south_nb)
        projs, projs16 = polar_factor_t(jnp.swapaxes(jnp.stack([lower + upper_nb, lower_nb + upper]), 1, 2))
        below_t = projs[0]
        above_t = projs[1]
        new_up = jnp.dot(above_t, upper, precision=lax.Precision.HIGH)
        new_low = jnp.dot(below_t, lower, precision=lax.Precision.HIGH)
        new_up = unit_scaled(new_up).astype(jnp.bfloat16)
        new_low = unit_scaled(new_low).astype(jnp.bfloat16)
        if step + 1 < STEPS:
            up_corner_nb = shifted(new_up, 1, -1)
            low_corner_nb = shifted(new_low, 1, 1)
        edge_new = edge_contract(west_edge, projs16[0], projs16[1], site)
        edge_new = unit_scaled(edge_new).astype(jnp.bfloat16)
        corner_up, west_edge, corner_low = shifted((new_up, edge_new, new_low), 1, 0)
    return (corner_up[None, None], west_edge[None, None], corner_low[None, None])


def solution(mesh):
    return jax.shard_map(
        per_device,
        mesh=mesh,
        in_specs=(
            P("gx", "gy", None, None),
            P("gx", "gy", None, None),
            P("gx", "gy", None, None),
            P("gx", "gy", None, None),
            P("gx", "gy", None, None),
            P("gx", "gy", None, None),
            P(),
            P(),
        ),
        out_specs=(P("gx", "gy", None, None), P("gx", "gy", None, None), P("gx", "gy", None, None)),
        check_vma=False,
    )
```

```python
import math

import jax
import jax.numpy as jnp
from jax import lax
from jax.experimental import pallas as pl
from jax.experimental.pallas import tpu as pltpu
from jax.sharding import PartitionSpec as P

NS_ITERS = 6
STEPS = 2
LANES = 128


def passed_along(shard, axis, by):
    peers = lax.axis_size(axis)
    return lax.ppermute(shard, axis, [(i, (i + by) % peers) for i in range(peers)])


def split_bf16(x):
    hi = x.astype(jnp.bfloat16)
    return hi, (x - hi.astype(jnp.float32)).astype(jnp.bfloat16)


def dot3(a, b, dims):
    ah, al = split_bf16(a)
    bh, bl = split_bf16(b)
    out = lambda p, q: lax.dot_general(p, q, (dims, ((), ())), preferred_element_type=jnp.float32)
    return out(ah, bh) + (out(ah, bl) + out(al, bh))


def gram3(y):
    yh, yl = split_bf16(y)
    out = lambda p, q: lax.dot_general(p, q, (((1,), (1,)), ((), ())), preferred_element_type=jnp.float32)
    cross = out(yh, yl)
    return out(yh, yh) + (cross + cross.T)


def polar_kernel(y_ref, o_ref, h_ref):
    count = y_ref.shape[0]
    ys = []
    for b in range(count):
        y = y_ref[b]
        ys.append(y / jnp.sqrt(jnp.sum(y * y) + 1e-06))
    for sweep in range(NS_ITERS):
        grams = [gram3(y) for y in ys]
        ys = [1.5 * y - 0.5 * dot3(g, y, ((1,), (0,))) for g, y in zip(grams, ys)]
    for b in range(count):
        o_ref[b] = ys[b]
        h_ref[b] = ys[b].astype(h_ref.dtype)


def polar_factor_t(stack):
    return pl.pallas_call(
        polar_kernel,
        out_shape=(
            jax.ShapeDtypeStruct(stack.shape, jnp.float32),
            jax.ShapeDtypeStruct(stack.shape, jnp.bfloat16),
        ),
        compiler_params=pltpu.CompilerParams(vmem_limit_bytes=32 * 1024 * 1024),
    )(stack)


def shifted(tree, dx, dy):
    nx = lax.axis_size("gx")
    ny = lax.axis_size("gy")
    pairs = []
    for x in range(nx):
        for y in range(ny):
            pairs.append((x * ny + y, ((x + dx) % nx) * ny + (y + dy) % ny))
    return lax.ppermute(tree, ("gx", "gy"), pairs)


def unit_scaled(tensor):
    return tensor / jnp.sqrt(jnp.mean(tensor * tensor) + 1e-06)


def edge_kernel(wd_ref, pm_ref, t_ref, qt_ref, o_ref, f_ref, g_ref):
    n = qt_ref.shape[0]
    dd = o_ref.shape[0]
    group = 4
    wd = wd_ref[...]
    for d0 in range(0, dd, group):
        part = jnp.dot(wd, pm_ref[:, d0 * LANES:(d0 + group) * LANES], preferred_element_type=jnp.float32)
        part = part.astype(jnp.bfloat16)
        for k in range(group):
            f_ref[:, d0 + k] = part[:, k * LANES:(k + 1) * LANES].reshape(n, dd, LANES)
    t = t_ref[...]
    per = n

    def mid_body(h, carry):
        x = jnp.concatenate([f_ref[h * per + k].reshape(dd * dd, LANES) for k in range(per)], axis=1)
        g = jnp.dot(t, x, preferred_element_type=jnp.float32).astype(jnp.bfloat16)
        for k in range(per):
            at = pl.multiple_of((h * per + k) * dd, dd)
            for r in range(dd):
                g_ref[pl.ds(at, dd), r * LANES:(r + 1) * LANES] = g[r * dd:(r + 1) * dd, k * LANES:(k + 1) * LANES]
        return carry

    lax.fori_loop(0, n // per, mid_body, 0)
    qt = qt_ref[...]
    for r0 in range(0, dd, group):
        part = jnp.dot(qt, g_ref[:, r0 * LANES:(r0 + group) * LANES], preferred_element_type=jnp.float32)
        for k in range(group):
            o_ref[r0 + k] = part[:, k * LANES:(k + 1) * LANES]


def edge_contract(west, low_t, up_t, site):
    n = west.shape[0]
    dd = west.shape[1] // n
    wd = west.reshape(n * dd, n)
    pm = jnp.transpose(low_t.reshape(n, n, dd), (1, 2, 0))
    pm = jnp.pad(pm, ((0, 0), (0, 0), (0, LANES - n))).reshape(n, dd * LANES)
    qt = up_t
    out = pl.pallas_call(
        edge_kernel,
        out_shape=jax.ShapeDtypeStruct((dd, n, LANES), jnp.float32),
        scratch_shapes=[
            pltpu.VMEM((n, dd, dd, LANES), jnp.bfloat16),
            pltpu.VMEM((n * dd, dd * LANES), jnp.bfloat16),
        ],
        compiler_params=pltpu.CompilerParams(vmem_limit_bytes=48 * 1024 * 1024),
    )(wd, pm, site, qt)
    return jnp.transpose(out[:, :, :n], (1, 0, 2)).reshape(n, dd * n)


def one_hot(rows, cols, row_key, col_key):
    r = lax.broadcasted_iota(jnp.int32, (rows, cols), 0)
    c = lax.broadcasted_iota(jnp.int32, (rows, cols), 1)
    return (row_key(r) == col_key(c)).astype(jnp.float32)


def double_layer(ket, bra):
    q = ket.shape[1]
    dd = q * q
    size = dd * dd
    ket_m = jnp.transpose(ket.astype(jnp.float32), (0, 3, 2, 4, 1)).reshape(ket.shape[0], dd, dd)
    bra_m = jnp.transpose(bra.astype(jnp.float32), (0, 3, 2, 4, 1)).reshape(bra.shape[0], dd, dd)
    k_row = one_hot(size, dd, lambda r: (r // (q * dd)) * q + (r // q) % q, lambda c: c)
    b_row = one_hot(size, dd, lambda r: ((r // dd) % q) * q + r % q, lambda c: c)
    k_col = one_hot(dd, size, lambda r: r, lambda c: (c // (q * dd)) * q + (c // q) % q)
    b_col = one_hot(dd, size, lambda r: r, lambda c: ((c // dd) % q) * q + c % q)
    ket_wide = jnp.einsum("ra,sab,bc->src", k_row, ket_m, k_col)
    bra_wide = jnp.einsum("ra,sab,bc->src", b_row, bra_m, b_col)
    return jnp.sum(ket_wide * bra_wide, axis=0).astype(jnp.bfloat16)


def per_device(
    c_upper, edge_upper, edge_left, c_lower, edge_lower, site_ket, time_gate, quench_sites
):
    env_width = c_upper.shape[-1]
    double_bond = edge_upper.shape[-1] // env_width
    bond_dim = math.isqrt(double_bond)
    phys_dim = site_ket.shape[2]
    ket_sites = site_ket[0, 0].reshape(phys_dim, bond_dim, bond_dim, bond_dim, bond_dim)
    gram = jnp.dot(time_gate.T, time_gate, precision=lax.Precision.HIGHEST)
    gated = jnp.einsum(
        "st,tabcd->sabcd", gram, ket_sites.astype(jnp.float32), precision=lax.Precision.HIGHEST
    )
    own_index = lax.axis_index("gx") * lax.axis_size("gy") + lax.axis_index("gy")
    chosen = jnp.any(quench_sites == own_index)
    bra = jnp.where(chosen, gated, ket_sites.astype(jnp.float32)).astype(jnp.bfloat16)
    site = double_layer(ket_sites, bra)
    north_edge = edge_upper[0, 0]
    south_edge = edge_lower[0, 0]
    corner_up = c_upper[0, 0]
    west_edge = edge_left[0, 0]
    corner_low = c_lower[0, 0]
    up_corner_nb, north_nb = shifted((corner_up, north_edge), 0, -1)
    low_corner_nb, south_nb = shifted((corner_low, south_edge), 0, 1)
    n = env_width
    for step in range(STEPS):
        def half(corner, edge):
            return jnp.dot(corner, edge, preferred_element_type=jnp.float32).reshape(n * double_bond, n)

        upper = half(corner_up, north_edge)
        lower = half(corner_low, south_edge)
        upper_nb = half(up_corner_nb, north_nb)
        lower_nb = half(low_corner_nb, south_nb)
        projs, projs16 = polar_factor_t(jnp.swapaxes(jnp.stack([lower + upper_nb, lower_nb + upper]), 1, 2))
        below_t = projs[0]
        above_t = projs[1]
        new_up = jnp.dot(above_t, upper, precision=lax.Precision.HIGH)
        new_low = jnp.dot(below_t, lower, precision=lax.Precision.HIGH)
        new_up = unit_scaled(new_up).astype(jnp.bfloat16)
        new_low = unit_scaled(new_low).astype(jnp.bfloat16)
        if step + 1 < STEPS:
            up_corner_nb = shifted(new_up, 1, -1)
            low_corner_nb = shifted(new_low, 1, 1)
        edge_new = edge_contract(west_edge, projs16[0], projs16[1], site)
        edge_new = unit_scaled(edge_new).astype(jnp.bfloat16)
        corner_up, west_edge, corner_low = shifted((new_up, edge_new, new_low), 1, 0)
    return (corner_up[None, None], west_edge[None, None], corner_low[None, None])


def solution(mesh):
    return jax.shard_map(
        per_device,
        mesh=mesh,
        in_specs=(
            P("gx", "gy", None, None),
            P("gx", "gy", None, None),
            P("gx", "gy", None, None),
            P("gx", "gy", None, None),
            P("gx", "gy", None, None),
            P("gx", "gy", None, None),
            P(),
            P(),
        ),
        out_specs=(P("gx", "gy", None, None), P("gx", "gy", None, None), P("gx", "gy", None, None)),
        check_vma=False,
    )
```

```python
import math

import jax
import jax.numpy as jnp
from jax import lax
from jax.experimental import pallas as pl
from jax.experimental.pallas import tpu as pltpu
from jax.sharding import PartitionSpec as P

NS_ITERS = 6
STEPS = 2
LANES = 128


def passed_along(shard, axis, by):
    peers = lax.axis_size(axis)
    return lax.ppermute(shard, axis, [(i, (i + by) % peers) for i in range(peers)])


def split_bf16(x):
    hi = x.astype(jnp.bfloat16)
    return hi, (x - hi.astype(jnp.float32)).astype(jnp.bfloat16)


def dot3(a, b, dims):
    ah, al = split_bf16(a)
    bh, bl = split_bf16(b)
    out = lambda p, q: lax.dot_general(p, q, (dims, ((), ())), preferred_element_type=jnp.float32)
    return out(ah, bh) + (out(ah, bl) + out(al, bh))


def gram3(y):
    yh, yl = split_bf16(y)
    out = lambda p, q: lax.dot_general(p, q, (((1,), (1,)), ((), ())), preferred_element_type=jnp.float32)
    cross = out(yh, yl)
    return out(yh, yh) + (cross + cross.T)


def polar_kernel(y_ref, o_ref, h_ref):
    count = y_ref.shape[0]
    ys = []
    for b in range(count):
        y = y_ref[b]
        ys.append(y * lax.rsqrt(jnp.sum(y * y, keepdims=True) + 1e-06))
    for sweep in range(NS_ITERS):
        grams = [gram3(y) for y in ys]
        ys = [1.5 * y - 0.5 * dot3(g, y, ((1,), (0,))) for g, y in zip(grams, ys)]
    for b in range(count):
        o_ref[b] = ys[b]
        h_ref[b] = ys[b].astype(h_ref.dtype)


def polar_factor_t(stack):
    return pl.pallas_call(
        polar_kernel,
        out_shape=(
            jax.ShapeDtypeStruct(stack.shape, jnp.float32),
            jax.ShapeDtypeStruct(stack.shape, jnp.bfloat16),
        ),
        compiler_params=pltpu.CompilerParams(vmem_limit_bytes=32 * 1024 * 1024),
    )(stack)


def shifted(tree, dx, dy):
    nx = lax.axis_size("gx")
    ny = lax.axis_size("gy")
    pairs = []
    for x in range(nx):
        for y in range(ny):
            pairs.append((x * ny + y, ((x + dx) % nx) * ny + (y + dy) % ny))
    return lax.ppermute(tree, ("gx", "gy"), pairs)


def unit_scaled(tensor):
    return tensor / jnp.sqrt(jnp.mean(tensor * tensor) + 1e-06)


def edge_kernel(wd_ref, pm_ref, t_ref, qt_ref, o_ref, f_ref, g_ref):
    n = qt_ref.shape[0]
    dd = o_ref.shape[0]
    group = 4
    wd = wd_ref[...]
    for d0 in range(0, dd, group):
        part = jnp.dot(wd, pm_ref[:, d0 * LANES:(d0 + group) * LANES], preferred_element_type=jnp.float32)
        part = part.astype(jnp.bfloat16)
        for k in range(group):
            f_ref[:, d0 + k] = part[:, k * LANES:(k + 1) * LANES].reshape(n, dd, LANES)
    t = t_ref[...]
    per = n

    def mid_body(h, carry):
        x = jnp.concatenate([f_ref[h * per + k].reshape(dd * dd, LANES) for k in range(per)], axis=1)
        g = jnp.dot(t, x, preferred_element_type=jnp.float32).astype(jnp.bfloat16)
        for k in range(per):
            at = pl.multiple_of((h * per + k) * dd, dd)
            for r in range(dd):
                g_ref[pl.ds(at, dd), r * LANES:(r + 1) * LANES] = g[r * dd:(r + 1) * dd, k * LANES:(k + 1) * LANES]
        return carry

    lax.fori_loop(0, n // per, mid_body, 0)
    qt = qt_ref[...]
    for r0 in range(0, dd, group):
        part = jnp.dot(qt, g_ref[:, r0 * LANES:(r0 + group) * LANES], preferred_element_type=jnp.float32)
        for k in range(group):
            o_ref[r0 + k] = part[:, k * LANES:(k + 1) * LANES]


def edge_contract(west, low_t, up_t, site):
    n = west.shape[0]
    dd = west.shape[1] // n
    wd = west.reshape(n * dd, n)
    pm = jnp.transpose(low_t.reshape(n, n, dd), (1, 2, 0))
    pm = jnp.pad(pm, ((0, 0), (0, 0), (0, LANES - n))).reshape(n, dd * LANES)
    qt = up_t
    out = pl.pallas_call(
        edge_kernel,
        out_shape=jax.ShapeDtypeStruct((dd, n, LANES), jnp.float32),
        scratch_shapes=[
            pltpu.VMEM((n, dd, dd, LANES), jnp.bfloat16),
            pltpu.VMEM((n * dd, dd * LANES), jnp.bfloat16),
        ],
        compiler_params=pltpu.CompilerParams(vmem_limit_bytes=48 * 1024 * 1024),
    )(wd, pm, site, qt)
    return jnp.transpose(out[:, :, :n], (1, 0, 2)).reshape(n, dd * n)


def one_hot(rows, cols, row_key, col_key):
    r = lax.broadcasted_iota(jnp.int32, (rows, cols), 0)
    c = lax.broadcasted_iota(jnp.int32, (rows, cols), 1)
    return (row_key(r) == col_key(c)).astype(jnp.float32)


def double_layer(ket, bra):
    q = ket.shape[1]
    dd = q * q
    size = dd * dd
    ket_m = jnp.transpose(ket.astype(jnp.float32), (0, 3, 2, 4, 1)).reshape(ket.shape[0], dd, dd)
    bra_m = jnp.transpose(bra.astype(jnp.float32), (0, 3, 2, 4, 1)).reshape(bra.shape[0], dd, dd)
    k_row = one_hot(size, dd, lambda r: (r // (q * dd)) * q + (r // q) % q, lambda c: c)
    b_row = one_hot(size, dd, lambda r: ((r // dd) % q) * q + r % q, lambda c: c)
    k_col = one_hot(dd, size, lambda r: r, lambda c: (c // (q * dd)) * q + (c // q) % q)
    b_col = one_hot(dd, size, lambda r: r, lambda c: ((c // dd) % q) * q + c % q)
    hi = lax.Precision.HIGHEST
    ket_wide = jnp.einsum("ra,sab,bc->src", k_row, ket_m, k_col, precision=hi)
    bra_wide = jnp.einsum("ra,sab,bc->src", b_row, bra_m, b_col, precision=hi)
    return jnp.sum(ket_wide * bra_wide, axis=0).astype(jnp.bfloat16)


def per_device(
    c_upper, edge_upper, edge_left, c_lower, edge_lower, site_ket, time_gate, quench_sites
):
    env_width = c_upper.shape[-1]
    double_bond = edge_upper.shape[-1] // env_width
    bond_dim = math.isqrt(double_bond)
    phys_dim = site_ket.shape[2]
    ket_sites = site_ket[0, 0].reshape(phys_dim, bond_dim, bond_dim, bond_dim, bond_dim)
    gram = jnp.dot(time_gate.T, time_gate, precision=lax.Precision.HIGHEST)
    gated = jnp.einsum(
        "st,tabcd->sabcd", gram, ket_sites.astype(jnp.float32), precision=lax.Precision.HIGHEST
    )
    own_index = lax.axis_index("gx") * lax.axis_size("gy") + lax.axis_index("gy")
    chosen = jnp.any(quench_sites == own_index)
    bra = jnp.where(chosen, gated, ket_sites.astype(jnp.float32)).astype(jnp.bfloat16)
    site = double_layer(ket_sites, bra)
    north_edge = edge_upper[0, 0]
    south_edge = edge_lower[0, 0]
    corner_up = c_upper[0, 0]
    west_edge = edge_left[0, 0]
    corner_low = c_lower[0, 0]
    up_corner_nb, north_nb = shifted((corner_up, north_edge), 0, -1)
    low_corner_nb, south_nb = shifted((corner_low, south_edge), 0, 1)
    n = env_width
    for step in range(STEPS):
        def half(corner, edge):
            return jnp.dot(corner, edge, preferred_element_type=jnp.float32).reshape(n * double_bond, n)

        upper = half(corner_up, north_edge)
        lower = half(corner_low, south_edge)
        upper_nb = half(up_corner_nb, north_nb)
        lower_nb = half(low_corner_nb, south_nb)
        projs, projs16 = polar_factor_t(jnp.swapaxes(jnp.stack([lower + upper_nb, lower_nb + upper]), 1, 2))
        below_t = projs[0]
        above_t = projs[1]
        new_up = jnp.dot(above_t, upper, precision=lax.Precision.HIGH)
        new_low = jnp.dot(below_t, lower, precision=lax.Precision.HIGH)
        new_up = unit_scaled(new_up).astype(jnp.bfloat16)
        new_low = unit_scaled(new_low).astype(jnp.bfloat16)
        if step + 1 < STEPS:
            up_corner_nb = shifted(new_up, 1, -1)
            low_corner_nb = shifted(new_low, 1, 1)
        edge_new = edge_contract(west_edge, projs16[0], projs16[1], site)
        edge_new = unit_scaled(edge_new).astype(jnp.bfloat16)
        corner_up, west_edge, corner_low = shifted((new_up, edge_new, new_low), 1, 0)
    return (corner_up[None, None], west_edge[None, None], corner_low[None, None])


def solution(mesh):
    return jax.shard_map(
        per_device,
        mesh=mesh,
        in_specs=(
            P("gx", "gy", None, None),
            P("gx", "gy", None, None),
            P("gx", "gy", None, None),
            P("gx", "gy", None, None),
            P("gx", "gy", None, None),
            P("gx", "gy", None, None),
            P(),
            P(),
        ),
        out_specs=(P("gx", "gy", None, None), P("gx", "gy", None, None), P("gx", "gy", None, None)),
        check_vma=False,
    )
```
